128 devices in a mesh: gx: 8 (over x, core), gy: 16 (over z, y).
Axes of the slice: x: 4, y: 4, z: 4, core: 2. Of those that a mesh axis runs over, the one named last changes fastest.
Arguments:
- start_disp: float32 [3, 256, 512, 128], P(None, 'gx', 'gy'), may hold values from -6 to 6
- start_vel: float32 [3, 256, 512, 128], P(None, 'gx', 'gy'), may hold values from -6 to 6
- stiffness: float32 [256, 512, 128], P('gx', 'gy'), may hold values from 0.5 to 2
- cell_mass: float32 [256, 512, 128], P('gx', 'gy'), may hold values from 0.5 to 2
- contact_cells: int32 [8, 16, 512], P('gx', 'gy'), may hold values from 0 to 1023
- contact_match: int32 [8, 16, 512], P('gx', 'gy'), may hold values from 0 to 511, each once within a row
- eroded_cells: int32 [8, 8, 16, 512], P(None, 'gx', 'gy'), may hold values from 0 to 131071
- owner_ids: int32 [8, 8, 16, 512, 1], P(None, 'gx', 'gy'), may hold values from 0 to 15; in each aligned block of 512 rows (0 to 511, 512 to 1023, ..., all dimensions but the last counted through in order) at most 128 rows name the same one
- bed_position: float32 [8, 16, 3, 2048], P('gx', 'gy'), may hold values from -6 to 6
- bed_velocity: float32 [8, 16, 3, 2048], P('gx', 'gy'), may hold values from -6 to 6
- bed_neighbours: int32 [8, 16, 8, 2048], P('gx', 'gy'), may hold values from 0 to 127
Outputs:
- final_disp: float32 [3, 256, 512, 128], P(None, 'gx', 'gy')
- final_vel: float32 [3, 256, 512, 128], P(None, 'gx', 'gy')
The draws below stay inside these ranges and needn't reach their ends.
Inputs may be any that keep to these rules, and one draw needn't show every extreme that they name: `owner_ids`: in each step, at most 128 records of one block name one owner, and some block names some owner exactly 128 times.
All inputs are finite; a program needn't handle non-finite values.
Results may differ from the reference program's by a relative error of at most 0.0001.
Values sent between devices are 32-bit elements; how exact they have to be, the bound alone decides.
No kernel may reach another device: no remote copies, remote signals or barrier semaphores. Data moves between devices by JAX's collectives and lax.ppermute only.
A program may use at most 128 MiB of HBM per device.

```python
import math
import jax
import jax.numpy as jnp
import numpy as np

CX = 32
CY = 32
NZ = 128
STEPS = 8
SEG = 512
ER = 512
CAP = 128
KNB = 8
NX = 256
NY = 512
PART = 2048
BLOCK = 128
N_GX = 8
N_GY = 16


def touch_ends(values, rng, low, high):
    longest = values.shape.index(max(values.shape))
    spots = []
    for shift in (0, 1):
        where = [jax.random.randint(jax.random.fold_in(rng, axis), (), 0, length) for axis, length in enumerate(values.shape)]
        where[longest] = (where[longest] + shift) % values.shape[longest]
        spots.append(tuple(where))
    return values.at[spots[0]].set(low).at[spots[1]].set(high)


def levels(rng, extent, split, smallest, high):
    level = 1.0
    for dim, parts in split:
        heights = jax.random.uniform(jax.random.fold_in(jax.random.fold_in(rng, 6), dim), (parts,), jnp.float32, smallest / len(split), high / len(split))
        level = level * jnp.repeat(jnp.exp(heights), extent[dim] // parts).reshape((-1,) + (1,) * (len(extent) - 1 - dim))
    return level


def shared_out(rng, own, number, rows, amount, top, limit, skew):
    ranking = jax.random.permutation(rng, amount)
    heavy_load, ordinary = shares(amount, rows * top, limit, skew, True), shares(amount, rows * top, limit, skew, False)
    places = jnp.arange(amount)

    def named(lengths, rotation):
        used = int((lengths > 0).sum())
        fixed = max(1, used // 4)
        passed = fixed + (places - fixed + rotation * (used - fixed)) % max(1, amount - fixed)
        return jnp.zeros((amount,), jnp.int32).at[ranking[jnp.where(places < fixed, places, passed)]].set(jnp.asarray(lengths, jnp.int32))

    lengths = jnp.where(number % 4 == 0, named(heavy_load, number // 4), named(ordinary, number - number // 4 - 1))
    mixed = jax.random.permutation(jax.random.fold_in(own, 3), amount)
    giver, receiver = mixed[0:amount // 2 * 2:2], mixed[1:amount // 2 * 2:2]
    slack = jnp.minimum(lengths[giver] - 1, limit - lengths[receiver]) // 2
    slack = jnp.where((giver == ranking[0]) | (receiver == ranking[0]) | (lengths[receiver] == 0), 0, jnp.maximum(slack, 0))
    passed = jax.random.randint(jax.random.fold_in(own, 4), (amount // 2,), 0, 1 << 20) % (slack + 1)
    lengths = lengths.at[giver].add(-passed).at[receiver].add(passed)
    items = jnp.searchsorted(jnp.cumsum(lengths), jnp.arange(rows * top), side="right").astype(jnp.int32)
    table = items.reshape(top, rows).T
    table = table[jax.random.permutation(jax.random.fold_in(own, 1), rows)]
    rotation = jax.random.randint(jax.random.fold_in(own, 2), (rows, 1), 0, top)
    return jnp.take_along_axis(table, (jnp.arange(top)[None, :] + rotation) % top, axis=1)


def shares(amount, total, most, skew, full):
    weights = [(1 << 20) // math.isqrt(grade ** skew) + 1 for grade in range(1, amount + 1)]
    largest = most if full else min(most, max(-(-total // amount), total * weights[0] // sum(weights)))
    least = 1 if total - largest >= amount - 1 else 0
    given, surplus = [largest] + [least] * (amount - 1), total - largest - least * (amount - 1)
    while surplus > 0:
        candidates = [i for i in range(1, amount) if given[i] < largest] or [i for i in range(1, amount) if given[i] < most]
        whole, budget = sum([weights[i] for i in candidates]), surplus
        for i in candidates:
            addition = min(most - given[i], max(1, budget * weights[i] // whole), surplus)
            given[i] = given[i] + addition
            surplus = surplus - addition
    return np.array(given)


def normal_values(rng, shape, deviation, most, split=(), held_as=jnp.bfloat16):
    factor_of = levels(rng, shape, split, -0.22, 0.18) if split else 1.0
    result = jax.random.normal(rng, shape, jnp.float32) * deviation * factor_of
    return jnp.minimum(jnp.maximum(result, -most), most).astype(held_as)


def setup_inputs(seed: int = 0) -> dict:
    key_of = jax.random.split(jax.random.key(seed), 12)
    start_disp = normal_values(key_of[0], (3, NX, NY, NZ), 1.0, 6.0, ((1, 8), (2, 16)), jnp.float32)
    start_vel = normal_values(key_of[1], (3, NX, NY, NZ), 1.0, 6.0, ((1, 8), (2, 16)), jnp.float32)
    stiffness = jnp.clip(jnp.exp(math.log(2.0) - 1.3862944 * jax.random.uniform(key_of[2], (NX, NY, NZ), jnp.float32) ** levels(key_of[2], (NX, NY, NZ), ((0, 8), (1, 16)), -0.2, 0.2)), 0.5, 2.0)
    cell_mass = jnp.clip(jnp.exp(math.log(2.0) - 1.3862944 * jax.random.uniform(key_of[3], (NX, NY, NZ), jnp.float32) ** levels(key_of[3], (NX, NY, NZ), ((0, 8), (1, 16)), -0.2, 0.2)), 0.5, 2.0)
    contact_cells = touch_ends(jax.random.randint(key_of[4], (N_GX, N_GY, SEG), 0, CX * CY), jax.random.fold_in(key_of[4], 1), 0, (CX * CY) - 1).astype(jnp.int32)
    contact_match = jax.vmap(lambda own: jax.random.permutation(own, SEG))(jax.random.split(key_of[5], N_GX * N_GY)).reshape((N_GX, N_GY, SEG)).astype(jnp.int32)
    eroded_cells = touch_ends(jax.random.randint(key_of[6], (STEPS, N_GX, N_GY, ER), 0, CX * CY * NZ), jax.random.fold_in(key_of[6], 1), 0, (CX * CY * NZ) - 1).astype(jnp.int32)
    owner_ids_keys = jax.random.split(jax.random.fold_in(key_of[7], 1), STEPS * N_GX * N_GY * ER // ER)
    owner_ids_turns = jax.random.permutation(jax.random.fold_in(key_of[7], 3), STEPS * N_GX * N_GY * ER // ER)
    owner_ids = jax.vmap(lambda own, number: shared_out(jax.random.fold_in(key_of[7], 2), own, number, ER, N_GY, 1, CAP, 2))(owner_ids_keys, owner_ids_turns).reshape((STEPS, N_GX, N_GY, ER, 1))
    bed_position = normal_values(key_of[8], (N_GX, N_GY, 3, PART), 1.0, 6.0, ((0, 8), (1, 16)), jnp.float32)
    bed_velocity = normal_values(key_of[9], (N_GX, N_GY, 3, PART), 1.0, 6.0, ((0, 8), (1, 16)), jnp.float32)
    bed_neighbours = touch_ends(jax.random.randint(key_of[10], (N_GX, N_GY, KNB, PART), 0, BLOCK), jax.random.fold_in(key_of[10], 1), 0, BLOCK - 1).astype(jnp.int32)
    return {"start_disp": start_disp, "start_vel": start_vel, "stiffness": stiffness, "cell_mass": cell_mass, "contact_cells": contact_cells, "contact_match": contact_match, "eroded_cells": eroded_cells, "owner_ids": owner_ids, "bed_position": bed_position, "bed_velocity": bed_velocity, "bed_neighbours": bed_neighbours}


TIME_STEP = 0.2
CONTACT_K = 0.5
PARTICLE_K = 1.0
DRAG_COEF = 0.5


def to_blocks(field):
    comps = field.shape[0]
    return field.reshape(comps, N_GX, CX, N_GY, CY, NZ).transpose(1, 3, 0, 2, 4, 5).reshape(N_GX, N_GY, comps, CX * CY * NZ)


def from_blocks(blocks):
    comps = blocks.shape[2]
    return blocks.reshape(N_GX, N_GY, comps, CX, CY, NZ).transpose(2, 0, 3, 1, 4, 5).reshape(comps, NX, NY, NZ)


def add_rows(field, where, values):
    return field.at[:, where].add(values)


def reference(start_disp, start_vel, stiffness, cell_mass, contact_cells, contact_match, eroded_cells, owner_ids, bed_position, bed_velocity, bed_neighbours):
    displace = start_disp
    velocity = start_vel
    part_pos = bed_position
    part_vel = bed_velocity
    gx_index = jnp.arange(N_GX, dtype=jnp.int32)[:, None, None]
    gy_index = jnp.arange(N_GY, dtype=jnp.int32)[None, :, None]
    slot_row = jnp.arange(PART, dtype=jnp.int32)
    nbr_rows = (slot_row // BLOCK) * BLOCK + bed_neighbours
    mass_blocks = to_blocks(cell_mass[None])[:, :, 0]
    surf_cells = contact_cells * NZ + (NZ - 1)
    adder = jax.vmap(jax.vmap(add_rows))
    for step_id in range(STEPS):
        padded = jnp.pad(displace, ((0, 0), (1, 1), (1, 1), (1, 1)))
        laplace = padded[:, 2:, 1:-1, 1:-1] + padded[:, :-2, 1:-1, 1:-1] + padded[:, 1:-1, 2:, 1:-1] + padded[:, 1:-1, :-2, 1:-1]
        laplace = laplace + (padded[:, 1:-1, 1:-1, 2:] + padded[:, 1:-1, 1:-1, :-2]) - 6.0 * displace
        internal = stiffness[None] * laplace
        force_blocks = to_blocks(internal)
        disp_blocks = to_blocks(displace)
        vel_blocks = to_blocks(velocity)
        seg_rows = jnp.take_along_axis(disp_blocks, surf_cells[:, :, None, :], axis=3)
        partner = seg_rows[jnp.arange(N_GX) ^ 1]
        facing = jnp.take_along_axis(partner, contact_match[:, :, None, :], axis=3)
        force_blocks = adder(force_blocks, surf_cells, CONTACT_K * (facing - seg_rows))
        cells_now = eroded_cells[step_id]
        owners_now = owner_ids[step_id, :, :, :, 0]
        is_owner = owners_now[..., None] == jnp.arange(N_GY, dtype=jnp.int32)
        counted = jnp.cumsum(is_owner.astype(jnp.int32), axis=2)
        slot_rank = jnp.sum(jnp.where(is_owner, counted, 0), axis=-1) - 1
        slot_id = slot_rank * N_GY + gy_index
        rec_mass = jnp.take_along_axis(mass_blocks, cells_now, axis=2)
        rec_disp = jnp.take_along_axis(disp_blocks, cells_now[:, :, None, :], axis=3)
        rec_mom = rec_mass[:, :, None, :] * jnp.take_along_axis(vel_blocks, cells_now[:, :, None, :], axis=3)
        nbr_cells = nbr_rows[gx_index, owners_now, :, slot_id]
        bed_near = part_pos[gx_index[..., None], owners_now[..., None], :, nbr_cells]
        bed_drift = part_vel[gx_index[..., None], owners_now[..., None], :, nbr_cells]
        offset = bed_near - rec_disp.transpose(0, 1, 3, 2)[:, :, :, None, :]
        weights = 1.0 / (1.0 + jnp.sum(offset * offset, axis=-1))
        mass_col = rec_mass[:, :, :, None, None]
        mom_col = rec_mom.transpose(0, 1, 3, 2)[:, :, :, None, :]
        spring = weights[..., None] * (PARTICLE_K * mass_col * offset)
        terms = spring + weights[..., None] * (DRAG_COEF * (mass_col * bed_drift - mom_col))
        rec_force = jnp.sum(terms, axis=3) / KNB
        force_blocks = adder(force_blocks, cells_now, rec_force.transpose(0, 1, 3, 2))
        part_vel = part_vel.at[gx_index[..., None], owners_now[..., None], :, nbr_cells].add(-TIME_STEP * spring / KNB)
        part_pos = part_pos + TIME_STEP * part_vel
        forces = from_blocks(force_blocks)
        velocity = velocity + TIME_STEP * (forces / cell_mass[None])
        displace = displace + TIME_STEP * velocity
    return displace, velocity
```

```python
import jax
import jax.numpy as jnp
from jax import lax
from jax.sharding import PartitionSpec as P

TIME_STEP = 0.2
CONTACT_K = 0.5
PARTICLE_K = 1.0
DRAG_COEF = 0.5
HIGHEST = lax.Precision.HIGHEST


def shift_pairs(axis, up):
    count = lax.axis_size(axis)
    if up:
        return [(i, i + 1) for i in range(count - 1)]
    return [(i + 1, i) for i in range(count - 1)]


def from_partner(value, axis, stride):
    mask = 2**stride
    pairs = [(source, source ^ mask) for source in range(lax.axis_size(axis))]
    return lax.ppermute(value, axis, pairs)


def split3(x):
    hi = lax.reduce_precision(x, exponent_bits=8, mantissa_bits=7)
    rest = x - hi
    mid = lax.reduce_precision(rest, exponent_bits=8, mantissa_bits=7)
    lo = rest - mid
    return jnp.stack([hi, mid, lo]).astype(jnp.bfloat16)


def laplacian(d):
    xm_face = lax.ppermute(d[:, -1], "gx", shift_pairs("gx", True))
    xp_face = lax.ppermute(d[:, 0], "gx", shift_pairs("gx", False))
    ym_face = lax.ppermute(d[:, :, -1], "gy", shift_pairs("gy", True))
    yp_face = lax.ppermute(d[:, :, 0], "gy", shift_pairs("gy", False))
    xp = jnp.concatenate([d[:, 1:], xp_face[:, None]], axis=1)
    xm = jnp.concatenate([xm_face[:, None], d[:, :-1]], axis=1)
    yp = jnp.concatenate([d[:, :, 1:], yp_face[:, :, None]], axis=2)
    ym = jnp.concatenate([ym_face[:, :, None], d[:, :, :-1]], axis=2)
    zeros = jnp.zeros_like(d[..., :1])
    zp = jnp.concatenate([d[..., 1:], zeros], axis=-1)
    zm = jnp.concatenate([zeros, d[..., :-1]], axis=-1)
    lap = xp + xm + yp + ym
    return lap + (zp + zm) - 6.0 * d


def local(
    start_disp,
    start_vel,
    stiffness,
    cell_mass,
    contact_cells,
    contact_match,
    eroded_cells,
    owner_ids,
    bed_position,
    bed_velocity,
    bed_neighbours,
):
    cols_x = start_disp.shape[1]
    cols_y = start_disp.shape[2]
    layers = start_disp.shape[3]
    n_cols = cols_x * cols_y
    n_owner = lax.axis_size("gy")
    n_slots = bed_position.shape[3]
    capacity = n_slots // n_owner
    row_block = min(128, n_slots)
    n_blocks = n_slots // row_block
    n_nbr = bed_neighbours.shape[2]
    n_seg = contact_cells.shape[2]
    n_steps = eroded_cells.shape[0]
    lane = jnp.arange(layers, dtype=jnp.int32)

    cc = contact_cells[0, 0]
    match_hot = (
        contact_match[0, 0][:, None] == jnp.arange(n_seg, dtype=jnp.int32)[None, :]
    ).astype(jnp.float32)

    cells_all = eroded_cells[:, 0, 0]
    owners_all = owner_ids[:, 0, 0, :, 0]
    is_owner = owners_all[..., None] == jnp.arange(n_owner, dtype=jnp.int32)
    counted = jnp.cumsum(is_owner.astype(jnp.int32), axis=1)
    rank_all = jnp.sum(jnp.where(is_owner, counted, 0), axis=-1) - 1
    slot_all = owners_all * capacity + rank_all
    col_all = cells_all // layers
    z_all = cells_all % layers
    mass_cols = cell_mass.reshape(n_cols, layers)
    mass_all = jnp.sum(
        jnp.take(mass_cols, col_all, axis=0) * (z_all[..., None] == lane), axis=-1
    )
    upd_cols = jnp.concatenate([jnp.broadcast_to(cc, (n_steps, n_seg)), col_all], axis=1)
    flat_all = upd_cols[:, None, :] + n_cols * jnp.arange(3, dtype=jnp.int32)[None, :, None]
    upd_lane = jnp.concatenate(
        [jnp.full((n_steps, n_seg), layers - 1, jnp.int32), z_all], axis=1
    )

    local_nbr = bed_neighbours[0, 0].reshape(n_nbr, n_blocks, row_block).transpose(1, 0, 2)
    nbr_hot = (
        local_nbr.reshape(n_blocks, n_nbr * row_block)[..., None]
        == jnp.arange(row_block, dtype=jnp.int32)
    ).astype(jnp.bfloat16)

    part_pos = bed_position[0, 0]
    part_vel = bed_velocity[0, 0]
    displace = start_disp
    velocity = start_vel
    for step_id in range(n_steps):
        laplace = laplacian(displace)
        internal = stiffness[None] * laplace

        disp_flat = displace.reshape(3 * n_cols, layers)
        vel_flat = velocity.reshape(3 * n_cols, layers)
        flat_rows = flat_all[step_id]
        lane_hot = upd_lane[step_id][:, None] == lane
        picked = jnp.take(disp_flat, flat_rows.reshape(-1), axis=0).reshape(3, -1, layers)
        picked = jnp.sum(jnp.where(lane_hot[None], picked, 0.0), axis=-1)
        seg_rows = picked[:, :n_seg]
        rec_disp = picked[:, n_seg:]
        rec_rows = flat_rows[:, n_seg:].reshape(-1)
        rec_velo = jnp.take(vel_flat, rec_rows, axis=0).reshape(3, -1, layers)
        rec_velo = jnp.sum(jnp.where(lane_hot[None, n_seg:], rec_velo, 0.0), axis=-1)

        partner = from_partner(seg_rows, "gx", 0)
        facing = jnp.einsum("fi,ji->fj", partner, match_hot, precision=HIGHEST)
        pull = CONTACT_K * (facing - seg_rows)

        rec_mass = mass_all[step_id]
        rec_mom = rec_mass[None] * rec_velo
        records = jnp.concatenate(
            [rec_mass[None], rec_disp, rec_mom, jnp.zeros_like(rec_mass)[None]], axis=0
        )
        slot = slot_all[step_id]
        buckets = jnp.zeros((n_slots, 8), jnp.float32).at[slot].set(records.T)
        buckets = buckets.reshape(n_owner, capacity, 8)
        arrived = lax.all_to_all(buckets, "gy", split_axis=0, concat_axis=0, tiled=True)
        columns = arrived.transpose(2, 1, 0).reshape(8, n_slots)
        slot_mass = columns[0]

        state = jnp.concatenate([part_pos, part_vel], axis=0).reshape(6, n_blocks, row_block)
        state_split = split3(state).reshape(3 * 6, n_blocks, row_block)
        gathered = jnp.einsum(
            "pbs,bqs->pbq", state_split, nbr_hot, preferred_element_type=jnp.float32
        ).reshape(3, 6, n_blocks, n_nbr, row_block)
        gathered = gathered[0] + gathered[1] + gathered[2]
        gathered = gathered.transpose(0, 2, 1, 3).reshape(6, n_nbr, n_slots)
        bed_near = gathered[0:3]
        bed_drift = gathered[3:6]

        offset = bed_near - columns[1:4][:, None, :]
        weights = 1.0 / (1.0 + jnp.sum(offset * offset, axis=0))
        spring = weights[None] * (PARTICLE_K * slot_mass * offset)
        terms = spring + weights[None] * (
            DRAG_COEF * (slot_mass * bed_drift - columns[4:7][:, None, :])
        )
        slot_force = jnp.sum(terms, axis=1) / n_nbr
        returned = slot_force.reshape(3, capacity, n_owner).transpose(2, 1, 0)
        answers = lax.all_to_all(returned, "gy", split_axis=0, concat_axis=0, tiled=True)
        rec_force = answers.reshape(n_slots, 3)[slot].T

        change = (-TIME_STEP * spring / n_nbr).reshape(3, n_nbr, n_blocks, row_block)
        change = change.transpose(0, 2, 1, 3).reshape(3, n_blocks, n_nbr * row_block)
        change_split = split3(change).reshape(9, n_blocks, n_nbr * row_block)
        vel_add = jnp.einsum(
            "pbq,bqs->pbs", change_split, nbr_hot, preferred_element_type=jnp.float32
        ).reshape(3, 3, n_slots)
        vel_add = vel_add[0] + vel_add[1] + vel_add[2]
        part_vel = part_vel + vel_add
        part_pos = part_pos + TIME_STEP * part_vel

        values = jnp.concatenate([pull, rec_force], axis=1)
        rows = jnp.where(lane_hot[None], values[:, :, None], 0.0)
        extra = jnp.zeros((3 * n_cols, layers), jnp.float32).at[flat_rows.reshape(-1)].add(
            rows.reshape(-1, layers)
        )
        forces = internal + extra.reshape(3, cols_x, cols_y, layers)
        velocity = velocity + TIME_STEP * (forces / cell_mass[None])
        displace = displace + TIME_STEP * velocity
    return (displace, velocity)


def solution(mesh):
    return jax.shard_map(
        local,
        mesh=mesh,
        in_specs=(
            P(None, "gx", "gy", None),
            P(None, "gx", "gy", None),
            P("gx", "gy", None),
            P("gx", "gy", None),
            P("gx", "gy", None),
            P("gx", "gy", None),
            P(None, "gx", "gy", None),
            P(None, "gx", "gy", None, None),
            P("gx", "gy", None, None),
            P("gx", "gy", None, None),
            P("gx", "gy", None, None),
        ),
        out_specs=(P(None, "gx", "gy", None), P(None, "gx", "gy", None)),
        check_vma=False,
    )
```

```python
import jax
import jax.numpy as jnp
from jax import lax
from jax.sharding import PartitionSpec as P

TIME_STEP = 0.2
CONTACT_K = 0.5
PARTICLE_K = 1.0
DRAG_COEF = 0.5
HIGHEST = lax.Precision.HIGHEST


def padded_2(cells, sides, width):
    for axis, dim in sides:
        count = lax.axis_size(axis)
        ends = count - 1
        head = lax.slice_in_dim(cells, 0, width, axis=dim)
        tail = lax.slice_in_dim(cells, cells.shape[dim] - width, cells.shape[dim], axis=dim)
        cells = jnp.concatenate(
            [
                lax.ppermute(tail, axis, [(i, (i + 1) % count) for i in range(ends)]),
                cells,
                lax.ppermute(head, axis, [((i + 1) % count, i) for i in range(ends)]),
            ],
            axis=dim,
        )
    return cells


def from_partner(value, axis, stride):
    mask = 2**stride
    pairs = [(source, source ^ mask) for source in range(lax.axis_size(axis))]
    return lax.ppermute(value, axis, pairs)


def split3(x):
    hi = lax.reduce_precision(x, exponent_bits=8, mantissa_bits=7)
    rest = x - hi
    mid = lax.reduce_precision(rest, exponent_bits=8, mantissa_bits=7)
    lo = rest - mid
    return jnp.stack([hi, mid, lo]).astype(jnp.bfloat16)


def depth_sum(field):
    zeros = jnp.zeros_like(field[..., :1])
    upper = jnp.concatenate([field[..., 1:], zeros], axis=-1)
    lower = jnp.concatenate([zeros, field[..., :-1]], axis=-1)
    return upper + lower


def local(
    start_disp,
    start_vel,
    stiffness,
    cell_mass,
    contact_cells,
    contact_match,
    eroded_cells,
    owner_ids,
    bed_position,
    bed_velocity,
    bed_neighbours,
):
    cols_x = start_disp.shape[1]
    cols_y = start_disp.shape[2]
    layers = start_disp.shape[3]
    n_cols = cols_x * cols_y
    n_owner = lax.axis_size("gy")
    n_slots = bed_position.shape[3]
    capacity = n_slots // n_owner
    row_block = min(128, n_slots)
    n_blocks = n_slots // row_block
    n_nbr = bed_neighbours.shape[2]
    n_seg = contact_cells.shape[2]
    n_rec = eroded_cells.shape[3]
    col_range = jnp.arange(n_cols, dtype=jnp.int32)
    layer_range = jnp.arange(layers, dtype=jnp.int32)
    seg_hot = (contact_cells[0, 0][:, None] == col_range[None, :]).astype(jnp.float32)
    match_hot = (
        contact_match[0, 0][:, None] == jnp.arange(n_seg, dtype=jnp.int32)[None, :]
    ).astype(jnp.float32)
    local_nbr = bed_neighbours[0, 0].reshape(n_nbr, n_blocks, row_block).transpose(1, 0, 2)
    nbr_hot = (
        local_nbr.reshape(n_blocks, n_nbr * row_block)[..., None]
        == jnp.arange(row_block, dtype=jnp.int32)
    ).astype(jnp.bfloat16)
    nbr_hot = lax.optimization_barrier(nbr_hot)
    owner_range = jnp.arange(n_owner, dtype=jnp.int32)
    rank_range = jnp.arange(capacity, dtype=jnp.int32)
    owners_all = owner_ids[:, 0, 0, :, 0]
    owner_hit = owners_all[..., None] == owner_range
    counted_all = jnp.cumsum(owner_hit.astype(jnp.int32), axis=1)
    rank_all = jnp.sum(jnp.where(owner_hit, counted_all, 0), axis=-1) - 1
    is_owner_all = owner_hit.astype(jnp.float32)
    rank_hot_all = (rank_all[..., None] == rank_range).astype(jnp.float32)
    mass_cols = cell_mass.reshape(n_cols, layers)
    part_pos = bed_position[0, 0]
    part_vel = bed_velocity[0, 0]
    displace = start_disp
    velocity = start_vel
    for step_id in range(eroded_cells.shape[0]):
        padded = padded_2(displace, (("gx", 1), ("gy", 2)), 1)
        laplace = (
            padded[:, 2:, 1:-1] + padded[:, :-2, 1:-1] + padded[:, 1:-1, 2:] + padded[:, 1:-1, :-2]
        )
        laplace = laplace + depth_sum(displace) - 6.0 * displace
        internal = stiffness[None] * laplace
        forces = internal.reshape(3, n_cols, layers)
        disp_cols = displace.reshape(3, n_cols, layers)
        vel_cols = velocity.reshape(3, n_cols, layers)
        top_layer = disp_cols[:, :, layers - 1]
        seg_rows = jnp.einsum("fc,jc->fj", top_layer, seg_hot, precision=HIGHEST)
        partner = from_partner(seg_rows, "gx", 0)
        facing = jnp.einsum("fi,ji->fj", partner, match_hot, precision=HIGHEST)
        top_add = jnp.einsum(
            "fj,jc->fc", CONTACT_K * (facing - seg_rows), seg_hot, precision=HIGHEST
        )
        forces = forces.at[:, :, layers - 1].add(top_add)
        cells_now = eroded_cells[step_id, 0, 0]
        col_hot = ((cells_now // layers)[:, None] == col_range[None, :]).astype(jnp.float32)
        layer_hot = ((cells_now % layers)[:, None] == layer_range[None, :]).astype(jnp.float32)
        stacked = jnp.concatenate([mass_cols[None], disp_cols, vel_cols], axis=0)
        picked_cols = jnp.einsum("fcz,ec->fez", stacked, col_hot, precision=HIGHEST)
        picked = jnp.sum(picked_cols * layer_hot[None], axis=2)
        rec_mass = picked[0]
        rec_disp = picked[1:4]
        rec_mom = rec_mass[None] * picked[4:7]
        is_owner = is_owner_all[step_id]
        rank_hot = rank_hot_all[step_id]
        state = jnp.concatenate([part_pos, part_vel], axis=0).reshape(6, n_blocks, row_block)
        state_split = split3(state).reshape(3 * 6, n_blocks, row_block)
        gathered = jnp.einsum(
            "pbs,bqs->pbq", state_split, nbr_hot, preferred_element_type=jnp.float32
        ).reshape(3, 6, n_blocks, n_nbr, row_block)
        gathered = gathered[0] + gathered[1] + gathered[2]
        gathered = gathered.transpose(0, 2, 1, 3).reshape(6, n_nbr, n_slots)
        bed_near = gathered[0:3]
        bed_drift = gathered[3:6]
        records = jnp.concatenate([rec_mass[None], rec_disp, rec_mom], axis=0)
        buckets = jnp.einsum("eo,fe,er->ofr", is_owner, records, rank_hot, precision=HIGHEST)
        arrived = lax.all_to_all(buckets, "gy", split_axis=0, concat_axis=0, tiled=True)
        columns = arrived.transpose(1, 2, 0).reshape(7, n_slots)
        slot_mass = columns[0]
        offset = bed_near - columns[1:4][:, None, :]
        weights = 1.0 / (1.0 + jnp.sum(offset * offset, axis=0))
        spring = weights[None] * (PARTICLE_K * slot_mass * offset)
        terms = spring + weights[None] * (
            DRAG_COEF * (slot_mass * bed_drift - columns[4:7][:, None, :])
        )
        slot_force = jnp.sum(terms, axis=1) / n_nbr
        returned = slot_force.reshape(3, capacity, n_owner).transpose(2, 0, 1)
        answers = lax.all_to_all(returned, "gy", split_axis=0, concat_axis=0, tiled=True)
        rec_force = jnp.einsum("ofr,er,eo->fe", answers, rank_hot, is_owner, precision=HIGHEST)
        change = (-TIME_STEP * spring / n_nbr).reshape(3, n_nbr, n_blocks, row_block)
        change = change.transpose(0, 2, 1, 3).reshape(3, n_blocks, n_nbr * row_block)
        change_split = split3(change).reshape(9, n_blocks, n_nbr * row_block)
        vel_add = jnp.einsum(
            "pbq,bqs->pbs", change_split, nbr_hot, preferred_element_type=jnp.float32
        ).reshape(3, 3, n_slots)
        vel_add = vel_add[0] + vel_add[1] + vel_add[2]
        part_vel = part_vel + vel_add
        part_pos = part_pos + TIME_STEP * part_vel
        rec_add = jnp.einsum("ec,fe,ez->fcz", col_hot, rec_force, layer_hot, precision=HIGHEST)
        forces = (forces + rec_add).reshape(3, cols_x, cols_y, layers)
        velocity = velocity + TIME_STEP * (forces / cell_mass[None])
        displace = displace + TIME_STEP * velocity
    return (displace, velocity)


def solution(mesh):
    return jax.shard_map(
        local,
        mesh=mesh,
        in_specs=(
            P(None, "gx", "gy", None),
            P(None, "gx", "gy", None),
            P("gx", "gy", None),
            P("gx", "gy", None),
            P("gx", "gy", None),
            P("gx", "gy", None),
            P(None, "gx", "gy", None),
            P(None, "gx", "gy", None, None),
            P("gx", "gy", None, None),
            P("gx", "gy", None, None),
            P("gx", "gy", None, None),
        ),
        out_specs=(P(None, "gx", "gy", None), P(None, "gx", "gy", None)),
        check_vma=False,
    )
```

```python
import jax
import jax.numpy as jnp
from jax import lax
from jax.experimental import pallas as pl
from jax.experimental.pallas import tpu as pltpu
from jax.sharding import PartitionSpec as P

TIME_STEP = 0.2
CONTACT_K = 0.5
PARTICLE_K = 1.0
DRAG_COEF = 0.5
HIGHEST = lax.Precision.HIGHEST


def padded_2(cells, sides, width):
    for axis, dim in sides:
        count = lax.axis_size(axis)
        ends = count - 1
        head = lax.slice_in_dim(cells, 0, width, axis=dim)
        tail = lax.slice_in_dim(cells, cells.shape[dim] - width, cells.shape[dim], axis=dim)
        cells = jnp.concatenate(
            [
                lax.ppermute(tail, axis, [(i, (i + 1) % count) for i in range(ends)]),
                cells,
                lax.ppermute(head, axis, [((i + 1) % count, i) for i in range(ends)]),
            ],
            axis=dim,
        )
    return cells


def update_kernel(d_ref, v_ref, st_ref, m_ref, xm_ref, xp_ref, ym_ref, yp_ref,
                  cols_ref, lanes_ref, vals_ref, dn_ref, vn_ref, hot_ref):
    cx, cy, nz = d_ref.shape[1], d_ref.shape[2], d_ref.shape[3]
    n_cols = cx * cy
    n_ent = cols_ref.shape[1]

    @pl.when(pl.program_id(0) == 0)
    def _():
        col_iota = lax.broadcasted_iota(jnp.int32, (n_cols, n_ent), 0)
        hot_ref[...] = (col_iota == cols_ref[...]).astype(jnp.bfloat16)

    d = d_ref[0]
    xp = jnp.concatenate([d[1:], xp_ref[0][None]], axis=0)
    xm = jnp.concatenate([xm_ref[0][None], d[:-1]], axis=0)
    y_iota = lax.broadcasted_iota(jnp.int32, (cx, cy, nz), 1)
    z_iota = lax.broadcasted_iota(jnp.int32, (cx, cy, nz), 2)
    yp = jnp.where(y_iota == cy - 1, yp_ref[0][:, None, :], pltpu.roll(d, cy - 1, 1))
    ym = jnp.where(y_iota == 0, ym_ref[0][:, None, :], pltpu.roll(d, 1, 1))
    zp = jnp.where(z_iota == nz - 1, 0.0, pltpu.roll(d, nz - 1, 2))
    zm = jnp.where(z_iota == 0, 0.0, pltpu.roll(d, 1, 2))
    lap = xp + xm + yp + ym
    lap = lap + (zp + zm) - 6.0 * d
    internal = st_ref[...] * lap

    lane_hit = lanes_ref[...] == lax.broadcasted_iota(jnp.int32, (n_ent, nz), 1)
    hot = hot_ref[...]
    extra = None
    for part in range(vals_ref.shape[1]):
        w = jnp.where(lane_hit, vals_ref[0, part], 0.0).astype(jnp.bfloat16)
        term = jnp.dot(hot, w, preferred_element_type=jnp.float32)
        extra = term if extra is None else extra + term
    forces = internal + extra.reshape(cx, cy, nz)
    vn = v_ref[0] + TIME_STEP * (forces / m_ref[...])
    vn_ref[0] = vn
    dn_ref[0] = d + TIME_STEP * vn


def update_call(d, v, st, m, xm, xp, ym, yp, cols, lanes, vals):
    comps, cx, cy, nz = d.shape
    n_ent = cols.shape[1]
    field = pl.BlockSpec((1, cx, cy, nz), lambda f: (f, 0, 0, 0))
    plane = pl.BlockSpec((cx, cy, nz), lambda f: (0, 0, 0))
    face = pl.BlockSpec((1, cx, nz), lambda f: (f, 0, 0))
    whole2 = lambda a: pl.BlockSpec(a.shape, lambda f: (0, 0))
    vals_spec = pl.BlockSpec((1,) + vals.shape[1:], lambda f: (f, 0, 0, 0))
    n_el = comps * cx * cy * nz
    cost = pl.CostEstimate(
        flops=int(2 * comps * vals.shape[1] * cx * cy * n_ent * nz + 20 * n_el),
        transcendentals=0,
        bytes_accessed=int(4 * (6 * n_el + 2 * cx * cy * nz)),
    )
    return pl.pallas_call(
        update_kernel,
        grid=(comps,),
        in_specs=[field, field, plane, plane, face, face, face, face,
                  whole2(cols), whole2(lanes), vals_spec],
        out_specs=[field, field],
        out_shape=[jax.ShapeDtypeStruct(d.shape, d.dtype)] * 2,
        scratch_shapes=[pltpu.VMEM((cx * cy, n_ent), jnp.bfloat16)],
        compiler_params=pltpu.CompilerParams(
            dimension_semantics=("arbitrary",), vmem_limit_bytes=48 * 1024 * 1024
        ),
        cost_estimate=cost,
    )(d, v, st, m, xm, xp, ym, yp, cols, lanes, vals)


def shift_pairs(axis, up):
    count = lax.axis_size(axis)
    if up:
        return [(i, i + 1) for i in range(count - 1)]
    return [(i + 1, i) for i in range(count - 1)]


def from_partner(value, axis, stride):
    mask = 2**stride
    pairs = [(source, source ^ mask) for source in range(lax.axis_size(axis))]
    return lax.ppermute(value, axis, pairs)


def split3(x):
    hi = lax.reduce_precision(x, exponent_bits=8, mantissa_bits=7)
    rest = x - hi
    mid = lax.reduce_precision(rest, exponent_bits=8, mantissa_bits=7)
    lo = rest - mid
    return jnp.stack([hi, mid, lo]).astype(jnp.bfloat16)


def depth_sum(field):
    zeros = jnp.zeros_like(field[..., :1])
    upper = jnp.concatenate([field[..., 1:], zeros], axis=-1)
    lower = jnp.concatenate([zeros, field[..., :-1]], axis=-1)
    return upper + lower


def local(
    start_disp,
    start_vel,
    stiffness,
    cell_mass,
    contact_cells,
    contact_match,
    eroded_cells,
    owner_ids,
    bed_position,
    bed_velocity,
    bed_neighbours,
):
    cols_x = start_disp.shape[1]
    cols_y = start_disp.shape[2]
    layers = start_disp.shape[3]
    n_cols = cols_x * cols_y
    n_owner = lax.axis_size("gy")
    n_slots = bed_position.shape[3]
    capacity = n_slots // n_owner
    row_block = min(128, n_slots)
    n_blocks = n_slots // row_block
    n_nbr = bed_neighbours.shape[2]
    n_seg = contact_cells.shape[2]
    n_rec = eroded_cells.shape[3]
    col_range = jnp.arange(n_cols, dtype=jnp.int32)
    layer_range = jnp.arange(layers, dtype=jnp.int32)
    seg_hot = (contact_cells[0, 0][:, None] == col_range[None, :]).astype(jnp.float32)
    match_hot = (
        contact_match[0, 0][:, None] == jnp.arange(n_seg, dtype=jnp.int32)[None, :]
    ).astype(jnp.float32)
    local_nbr = bed_neighbours[0, 0].reshape(n_nbr, n_blocks, row_block).transpose(1, 0, 2)
    nbr_hot = (
        local_nbr.reshape(n_blocks, n_nbr * row_block)[..., None]
        == jnp.arange(row_block, dtype=jnp.int32)
    ).astype(jnp.bfloat16)
    nbr_hot = lax.optimization_barrier(nbr_hot)
    owner_range = jnp.arange(n_owner, dtype=jnp.int32)
    rank_range = jnp.arange(capacity, dtype=jnp.int32)
    owners_all = owner_ids[:, 0, 0, :, 0]
    owner_hit = owners_all[..., None] == owner_range
    counted_all = jnp.cumsum(owner_hit.astype(jnp.int32), axis=1)
    rank_all = jnp.sum(jnp.where(owner_hit, counted_all, 0), axis=-1) - 1
    is_owner_all = owner_hit.astype(jnp.float32)
    rank_hot_all = (rank_all[..., None] == rank_range).astype(jnp.float32)
    mass_cols = cell_mass.reshape(n_cols, layers)
    n_steps = eroded_cells.shape[0]
    cells_all = eroded_cells[:, 0, 0]
    cc_all = jnp.broadcast_to(contact_cells[0, 0], (n_steps, n_seg))
    ent_cols = jnp.concatenate([cc_all, cells_all // layers], axis=1)[:, None, :]
    ent_lanes = jnp.concatenate(
        [jnp.full((n_steps, n_seg), layers - 1, jnp.int32), cells_all % layers], axis=1
    )[:, :, None]
    part_pos = bed_position[0, 0]
    part_vel = bed_velocity[0, 0]
    displace = start_disp
    velocity = start_vel
    for step_id in range(eroded_cells.shape[0]):
        xm_face = lax.ppermute(displace[:, -1], "gx", shift_pairs("gx", True))
        xp_face = lax.ppermute(displace[:, 0], "gx", shift_pairs("gx", False))
        ym_face = lax.ppermute(displace[:, :, -1], "gy", shift_pairs("gy", True))
        yp_face = lax.ppermute(displace[:, :, 0], "gy", shift_pairs("gy", False))
        disp_cols = displace.reshape(3, n_cols, layers)
        vel_cols = velocity.reshape(3, n_cols, layers)
        top_layer = disp_cols[:, :, layers - 1]
        seg_rows = jnp.einsum("fc,jc->fj", top_layer, seg_hot, precision=HIGHEST)
        partner = from_partner(seg_rows, "gx", 0)
        facing = jnp.einsum("fi,ji->fj", partner, match_hot, precision=HIGHEST)
        pull = CONTACT_K * (facing - seg_rows)
        cells_now = eroded_cells[step_id, 0, 0]
        col_hot = ((cells_now // layers)[:, None] == col_range[None, :]).astype(jnp.float32)
        layer_hot = ((cells_now % layers)[:, None] == layer_range[None, :]).astype(jnp.float32)
        stacked = jnp.concatenate([mass_cols[None], disp_cols, vel_cols], axis=0)
        picked_cols = jnp.einsum("fcz,ec->fez", stacked, col_hot, precision=HIGHEST)
        picked = jnp.sum(picked_cols * layer_hot[None], axis=2)
        rec_mass = picked[0]
        rec_disp = picked[1:4]
        rec_mom = rec_mass[None] * picked[4:7]
        is_owner = is_owner_all[step_id]
        rank_hot = rank_hot_all[step_id]
        state = jnp.concatenate([part_pos, part_vel], axis=0).reshape(6, n_blocks, row_block)
        state_split = split3(state).reshape(3 * 6, n_blocks, row_block)
        gathered = jnp.einsum(
            "pbs,bqs->pbq", state_split, nbr_hot, preferred_element_type=jnp.float32
        ).reshape(3, 6, n_blocks, n_nbr, row_block)
        gathered = gathered[0] + gathered[1] + gathered[2]
        gathered = gathered.transpose(0, 2, 1, 3).reshape(6, n_nbr, n_slots)
        bed_near = gathered[0:3]
        bed_drift = gathered[3:6]
        records = jnp.concatenate([rec_mass[None], rec_disp, rec_mom], axis=0)
        buckets = jnp.einsum("eo,fe,er->ofr", is_owner, records, rank_hot, precision=HIGHEST)
        arrived = lax.all_to_all(buckets, "gy", split_axis=0, concat_axis=0, tiled=True)
        columns = arrived.transpose(1, 2, 0).reshape(7, n_slots)
        slot_mass = columns[0]
        offset = bed_near - columns[1:4][:, None, :]
        weights = 1.0 / (1.0 + jnp.sum(offset * offset, axis=0))
        spring = weights[None] * (PARTICLE_K * slot_mass * offset)
        terms = spring + weights[None] * (
            DRAG_COEF * (slot_mass * bed_drift - columns[4:7][:, None, :])
        )
        slot_force = jnp.sum(terms, axis=1) / n_nbr
        returned = slot_force.reshape(3, capacity, n_owner).transpose(2, 0, 1)
        answers = lax.all_to_all(returned, "gy", split_axis=0, concat_axis=0, tiled=True)
        rec_force = jnp.einsum("ofr,er,eo->fe", answers, rank_hot, is_owner, precision=HIGHEST)
        change = (-TIME_STEP * spring / n_nbr).reshape(3, n_nbr, n_blocks, row_block)
        change = change.transpose(0, 2, 1, 3).reshape(3, n_blocks, n_nbr * row_block)
        change_split = split3(change).reshape(9, n_blocks, n_nbr * row_block)
        vel_add = jnp.einsum(
            "pbq,bqs->pbs", change_split, nbr_hot, preferred_element_type=jnp.float32
        ).reshape(3, 3, n_slots)
        vel_add = vel_add[0] + vel_add[1] + vel_add[2]
        part_vel = part_vel + vel_add
        part_pos = part_pos + TIME_STEP * part_vel
        values = jnp.concatenate([pull, rec_force], axis=1)
        values = split3(values).astype(jnp.float32).transpose(1, 0, 2)[..., None]
        displace, velocity = update_call(
            displace, velocity, stiffness, cell_mass, xm_face, xp_face, ym_face, yp_face,
            ent_cols[step_id], ent_lanes[step_id], values,
        )
    return (displace, velocity)


def solution(mesh):
    return jax.shard_map(
        local,
        mesh=mesh,
        in_specs=(
            P(None, "gx", "gy", None),
            P(None, "gx", "gy", None),
            P("gx", "gy", None),
            P("gx", "gy", None),
            P("gx", "gy", None),
            P("gx", "gy", None),
            P(None, "gx", "gy", None),
            P(None, "gx", "gy", None, None),
            P("gx", "gy", None, None),
            P("gx", "gy", None, None),
            P("gx", "gy", None, None),
        ),
        out_specs=(P(None, "gx", "gy", None), P(None, "gx", "gy", None)),
        check_vma=False,
    )
```

```python
import jax
import jax.numpy as jnp
from jax import lax
from jax.experimental import pallas as pl
from jax.experimental.pallas import tpu as pltpu
from jax.sharding import PartitionSpec as P

TIME_STEP = 0.2
CONTACT_K = 0.5
PARTICLE_K = 1.0
DRAG_COEF = 0.5
HIGHEST = lax.Precision.HIGHEST


def padded_2(cells, sides, width):
    for axis, dim in sides:
        count = lax.axis_size(axis)
        ends = count - 1
        head = lax.slice_in_dim(cells, 0, width, axis=dim)
        tail = lax.slice_in_dim(cells, cells.shape[dim] - width, cells.shape[dim], axis=dim)
        cells = jnp.concatenate(
            [
                lax.ppermute(tail, axis, [(i, (i + 1) % count) for i in range(ends)]),
                cells,
                lax.ppermute(head, axis, [((i + 1) % count, i) for i in range(ends)]),
            ],
            axis=dim,
        )
    return cells


def update_kernel(d_ref, v_ref, st_ref, m_ref, xm_ref, xp_ref, ym_ref, yp_ref,
                  cols_ref, lanes_ref, vals_ref, dn_ref, vn_ref, face_ref, hot_ref):
    cx, cy, nz = d_ref.shape[1], d_ref.shape[2], d_ref.shape[3]
    n_cols = cx * cy
    n_ent = cols_ref.shape[1]

    @pl.when(pl.program_id(0) == 0)
    def _():
        col_iota = lax.broadcasted_iota(jnp.int32, (n_cols, n_ent), 0)
        hot_ref[...] = (col_iota == cols_ref[...]).astype(jnp.bfloat16)

    d = d_ref[0]
    xp = jnp.concatenate([d[1:], xp_ref[0][None]], axis=0)
    xm = jnp.concatenate([xm_ref[0][None], d[:-1]], axis=0)
    y_iota = lax.broadcasted_iota(jnp.int32, (cx, cy, nz), 1)
    z_iota = lax.broadcasted_iota(jnp.int32, (cx, cy, nz), 2)
    yp = jnp.where(y_iota == cy - 1, yp_ref[0][:, None, :], pltpu.roll(d, cy - 1, 1))
    ym = jnp.where(y_iota == 0, ym_ref[0][:, None, :], pltpu.roll(d, 1, 1))
    zp = jnp.where(z_iota == nz - 1, 0.0, pltpu.roll(d, nz - 1, 2))
    zm = jnp.where(z_iota == 0, 0.0, pltpu.roll(d, 1, 2))
    lap = xp + xm + yp + ym
    lap = lap + (zp + zm) - 6.0 * d
    internal = st_ref[...] * lap

    lane_hit = lanes_ref[...] == lax.broadcasted_iota(jnp.int32, (nz, n_ent), 0)
    hot = hot_ref[...]
    extra = None
    for part in range(vals_ref.shape[1]):
        w = jnp.where(lane_hit, vals_ref[0, part], 0.0).astype(jnp.bfloat16)
        term = lax.dot_general(
            hot, w, (((1,), (1,)), ((), ())), preferred_element_type=jnp.float32
        )
        extra = term if extra is None else extra + term
    forces = internal + extra.reshape(cx, cy, nz)
    vn = v_ref[0] + TIME_STEP * (forces / m_ref[...])
    vn_ref[0] = vn
    dn = d + TIME_STEP * vn
    dn_ref[0] = dn
    face_ref[0, 0] = dn[0]
    face_ref[0, 1] = dn[cx - 1]
    face_ref[0, 2] = dn_ref[0, :, 0, :]
    face_ref[0, 3] = dn_ref[0, :, cy - 1, :]


def update_call(d, v, st, m, xm, xp, ym, yp, cols, lanes, vals):
    comps, cx, cy, nz = d.shape
    n_ent = cols.shape[1]
    field = pl.BlockSpec((1, cx, cy, nz), lambda f: (f, 0, 0, 0))
    plane = pl.BlockSpec((cx, cy, nz), lambda f: (0, 0, 0))
    face = pl.BlockSpec((1, cx, nz), lambda f: (f, 0, 0))
    whole2 = lambda a: pl.BlockSpec(a.shape, lambda f: (0, 0))
    vals_spec = pl.BlockSpec((1,) + vals.shape[1:], lambda f: (f, 0, 0, 0))
    n_el = comps * cx * cy * nz
    cost = pl.CostEstimate(
        flops=int(2 * comps * vals.shape[1] * cx * cy * n_ent * nz + 20 * n_el),
        transcendentals=0,
        bytes_accessed=int(4 * (6 * n_el + 2 * cx * cy * nz)),
    )
    return pl.pallas_call(
        update_kernel,
        grid=(comps,),
        in_specs=[field, field, plane, plane, face, face, face, face,
                  whole2(cols), whole2(lanes), vals_spec],
        out_specs=[field, field, pl.BlockSpec((1, 4, cx, nz), lambda f: (f, 0, 0, 0))],
        out_shape=[jax.ShapeDtypeStruct(d.shape, d.dtype)] * 2
        + [jax.ShapeDtypeStruct((comps, 4, cx, nz), d.dtype)],
        scratch_shapes=[pltpu.VMEM((cx * cy, n_ent), jnp.bfloat16)],
        compiler_params=pltpu.CompilerParams(
            dimension_semantics=("arbitrary",), vmem_limit_bytes=48 * 1024 * 1024
        ),
        cost_estimate=cost,
    )(d, v, st, m, xm, xp, ym, yp, cols, lanes, vals)


def shift_pairs(axis, up):
    count = lax.axis_size(axis)
    if up:
        return [(i, i + 1) for i in range(count - 1)]
    return [(i + 1, i) for i in range(count - 1)]


def from_partner(value, axis, stride):
    mask = 2**stride
    pairs = [(source, source ^ mask) for source in range(lax.axis_size(axis))]
    return lax.ppermute(value, axis, pairs)


def split3(x):
    hi = lax.reduce_precision(x, exponent_bits=8, mantissa_bits=7)
    rest = x - hi
    mid = lax.reduce_precision(rest, exponent_bits=8, mantissa_bits=7)
    lo = rest - mid
    return jnp.stack([hi, mid, lo]).astype(jnp.bfloat16)


def depth_sum(field):
    zeros = jnp.zeros_like(field[..., :1])
    upper = jnp.concatenate([field[..., 1:], zeros], axis=-1)
    lower = jnp.concatenate([zeros, field[..., :-1]], axis=-1)
    return upper + lower


def local(
    start_disp,
    start_vel,
    stiffness,
    cell_mass,
    contact_cells,
    contact_match,
    eroded_cells,
    owner_ids,
    bed_position,
    bed_velocity,
    bed_neighbours,
):
    cols_x = start_disp.shape[1]
    cols_y = start_disp.shape[2]
    layers = start_disp.shape[3]
    n_cols = cols_x * cols_y
    n_owner = lax.axis_size("gy")
    n_slots = bed_position.shape[3]
    capacity = n_slots // n_owner
    row_block = min(128, n_slots)
    n_blocks = n_slots // row_block
    n_nbr = bed_neighbours.shape[2]
    n_seg = contact_cells.shape[2]
    n_rec = eroded_cells.shape[3]
    col_range = jnp.arange(n_cols, dtype=jnp.int32)
    layer_range = jnp.arange(layers, dtype=jnp.int32)
    seg_hot = (contact_cells[0, 0][:, None] == col_range[None, :]).astype(jnp.float32)
    match_hot = (
        contact_match[0, 0][:, None] == jnp.arange(n_seg, dtype=jnp.int32)[None, :]
    ).astype(jnp.float32)
    local_nbr = bed_neighbours[0, 0].reshape(n_nbr, n_blocks, row_block).transpose(1, 0, 2)
    nbr_hot = (
        local_nbr.reshape(n_blocks, n_nbr * row_block)[..., None]
        == jnp.arange(row_block, dtype=jnp.int32)
    ).astype(jnp.bfloat16)
    nbr_hot = lax.optimization_barrier(nbr_hot)
    owner_range = jnp.arange(n_owner, dtype=jnp.int32)
    rank_range = jnp.arange(capacity, dtype=jnp.int32)
    owners_all = owner_ids[:, 0, 0, :, 0]
    owner_hit = owners_all[..., None] == owner_range
    rec_range = jnp.arange(owner_ids.shape[3], dtype=jnp.int32)
    lower_tri = (rec_range[None, :] <= rec_range[:, None]).astype(jnp.float32)
    counted_all = jnp.einsum(
        "ij,sjo->sio", lower_tri, owner_hit.astype(jnp.float32), precision=HIGHEST
    )
    rank_all = jnp.sum(jnp.where(owner_hit, counted_all, 0.0), axis=-1).astype(jnp.int32) - 1
    is_owner_all = owner_hit.astype(jnp.float32)
    rank_hot_all = (rank_all[..., None] == rank_range).astype(jnp.float32)
    mass_cols = cell_mass.reshape(n_cols, layers)
    n_steps = eroded_cells.shape[0]
    cells_all = eroded_cells[:, 0, 0]
    cc_all = jnp.broadcast_to(contact_cells[0, 0], (n_steps, n_seg))
    ent_cols = jnp.concatenate([cc_all, cells_all // layers], axis=1)[:, None, :]
    ent_lanes = jnp.concatenate(
        [jnp.full((n_steps, n_seg), layers - 1, jnp.int32), cells_all % layers], axis=1
    )[:, None, :]
    part_pos = bed_position[0, 0]
    part_vel = bed_velocity[0, 0]
    displace = start_disp
    velocity = start_vel
    faces = jnp.stack(
        [start_disp[:, 0], start_disp[:, -1], start_disp[:, :, 0], start_disp[:, :, -1]], axis=1
    )
    for step_id in range(eroded_cells.shape[0]):
        xm_face = lax.ppermute(faces[:, 1], "gx", shift_pairs("gx", True))
        xp_face = lax.ppermute(faces[:, 0], "gx", shift_pairs("gx", False))
        ym_face = lax.ppermute(faces[:, 3], "gy", shift_pairs("gy", True))
        yp_face = lax.ppermute(faces[:, 2], "gy", shift_pairs("gy", False))
        disp_cols = displace.reshape(3, n_cols, layers)
        vel_cols = velocity.reshape(3, n_cols, layers)
        top_layer = disp_cols[:, :, layers - 1]
        seg_rows = jnp.einsum("fc,jc->fj", top_layer, seg_hot, precision=HIGHEST)
        partner = from_partner(seg_rows, "gx", 0)
        facing = jnp.einsum("fi,ji->fj", partner, match_hot, precision=HIGHEST)
        pull = CONTACT_K * (facing - seg_rows)
        cells_now = eroded_cells[step_id, 0, 0]
        col_hot = ((cells_now // layers)[:, None] == col_range[None, :]).astype(jnp.float32)
        layer_hot = ((cells_now % layers)[:, None] == layer_range[None, :]).astype(jnp.float32)
        stacked = jnp.concatenate([mass_cols[None], disp_cols, vel_cols], axis=0)
        picked_cols = jnp.einsum("fcz,ec->fez", stacked, col_hot, precision=HIGHEST)
        picked = jnp.sum(picked_cols * layer_hot[None], axis=2)
        rec_mass = picked[0]
        rec_disp = picked[1:4]
        rec_mom = rec_mass[None] * picked[4:7]
        is_owner = is_owner_all[step_id]
        rank_hot = rank_hot_all[step_id]
        state = jnp.concatenate([part_pos, part_vel], axis=0).reshape(6, n_blocks, row_block)
        state_split = split3(state).reshape(3 * 6, n_blocks, row_block)
        gathered = jnp.einsum(
            "pbs,bqs->pbq", state_split, nbr_hot, preferred_element_type=jnp.float32
        ).reshape(3, 6, n_blocks, n_nbr, row_block)
        gathered = gathered[0] + gathered[1] + gathered[2]
        gathered = gathered.transpose(0, 2, 1, 3).reshape(6, n_nbr, n_slots)
        bed_near = gathered[0:3]
        bed_drift = gathered[3:6]
        records = jnp.concatenate([rec_mass[None], rec_disp, rec_mom], axis=0)
        buckets = jnp.einsum("eo,fe,er->ofr", is_owner, records, rank_hot, precision=HIGHEST)
        arrived = lax.all_to_all(buckets, "gy", split_axis=0, concat_axis=0, tiled=True)
        columns = arrived.transpose(1, 2, 0).reshape(7, n_slots)
        slot_mass = columns[0]
        offset = bed_near - columns[1:4][:, None, :]
        weights = 1.0 / (1.0 + jnp.sum(offset * offset, axis=0))
        spring = weights[None] * (PARTICLE_K * slot_mass * offset)
        terms = spring + weights[None] * (
            DRAG_COEF * (slot_mass * bed_drift - columns[4:7][:, None, :])
        )
        slot_force = jnp.sum(terms, axis=1) / n_nbr
        returned = slot_force.reshape(3, capacity, n_owner).transpose(2, 0, 1)
        answers = lax.all_to_all(returned, "gy", split_axis=0, concat_axis=0, tiled=True)
        rec_force = jnp.einsum("ofr,er,eo->fe", answers, rank_hot, is_owner, precision=HIGHEST)
        change = (-TIME_STEP * spring / n_nbr).reshape(3, n_nbr, n_blocks, row_block)
        change = change.transpose(0, 2, 1, 3).reshape(3, n_blocks, n_nbr * row_block)
        change_split = split3(change).reshape(9, n_blocks, n_nbr * row_block)
        vel_add = jnp.einsum(
            "pbq,bqs->pbs", change_split, nbr_hot, preferred_element_type=jnp.float32
        ).reshape(3, 3, n_slots)
        vel_add = vel_add[0] + vel_add[1] + vel_add[2]
        part_vel = part_vel + vel_add
        part_pos = part_pos + TIME_STEP * part_vel
        values = jnp.concatenate([pull, rec_force], axis=1)
        values = split3(values).astype(jnp.float32).transpose(1, 0, 2)[:, :, None, :]
        displace, velocity, faces = update_call(
            displace, velocity, stiffness, cell_mass, xm_face, xp_face, ym_face, yp_face,
            ent_cols[step_id], ent_lanes[step_id], values,
        )
    return (displace, velocity)


def solution(mesh):
    return jax.shard_map(
        local,
        mesh=mesh,
        in_specs=(
            P(None, "gx", "gy", None),
            P(None, "gx", "gy", None),
            P("gx", "gy", None),
            P("gx", "gy", None),
            P("gx", "gy", None),
            P("gx", "gy", None),
            P(None, "gx", "gy", None),
            P(None, "gx", "gy", None, None),
            P("gx", "gy", None, None),
            P("gx", "gy", None, None),
            P("gx", "gy", None, None),
        ),
        out_specs=(P(None, "gx", "gy", None), P(None, "gx", "gy", None)),
        check_vma=False,
    )
```

```python
import jax
import jax.numpy as jnp
from jax import lax
from jax.experimental import pallas as pl
from jax.experimental.pallas import tpu as pltpu
from jax.sharding import PartitionSpec as P

TIME_STEP = 0.2
CONTACT_K = 0.5
PARTICLE_K = 1.0
DRAG_COEF = 0.5
HIGHEST = lax.Precision.HIGHEST


def padded_2(cells, sides, width):
    for axis, dim in sides:
        count = lax.axis_size(axis)
        ends = count - 1
        head = lax.slice_in_dim(cells, 0, width, axis=dim)
        tail = lax.slice_in_dim(cells, cells.shape[dim] - width, cells.shape[dim], axis=dim)
        cells = jnp.concatenate(
            [
                lax.ppermute(tail, axis, [(i, (i + 1) % count) for i in range(ends)]),
                cells,
                lax.ppermute(head, axis, [((i + 1) % count, i) for i in range(ends)]),
            ],
            axis=dim,
        )
    return cells


def gather_rows(fields, ghot, zmask, out_ref):
    c, nz = ghot.shape[1], zmask.shape[1]
    ones = jnp.ones((8, nz), jnp.bfloat16)
    for idx, fld in enumerate(fields):
        flat = fld.reshape(c, nz)
        hi = flat.astype(jnp.bfloat16)
        rest = flat - hi.astype(jnp.float32)
        mid = rest.astype(jnp.bfloat16)
        lo = (rest - mid.astype(jnp.float32)).astype(jnp.bfloat16)
        acc = None
        for part in (hi, mid, lo):
            rows = jnp.dot(ghot, part, preferred_element_type=jnp.float32)
            masked = jnp.where(zmask, rows, 0.0).astype(jnp.bfloat16)
            red = lax.dot_general(
                ones, masked, (((1,), (1,)), ((), ())), preferred_element_type=jnp.float32
            )
            acc = red if acc is None else acc + red
        out_ref[0, idx] = acc


def build_ghot(gcol_ref, ghot_ref, n_cols):
    n_ent = gcol_ref.shape[0]
    col_iota = lax.broadcasted_iota(jnp.int32, (n_ent, n_cols), 1)
    ghot_ref[...] = (gcol_ref[:, 0:1] == col_iota).astype(jnp.bfloat16)


def gather_kernel(d_ref, v_ref, gcol_ref, g_ref, ghot_ref):
    cx, cy, nz = d_ref.shape[1], d_ref.shape[2], d_ref.shape[3]

    @pl.when(pl.program_id(0) == 0)
    def _():
        build_ghot(gcol_ref, ghot_ref, cx * cy)

    zmask = gcol_ref[:, 1:2] == lax.broadcasted_iota(jnp.int32, (gcol_ref.shape[0], nz), 1)
    gather_rows((d_ref[0], v_ref[0]), ghot_ref[...], zmask, g_ref)


def gather_call(d, v, gcol):
    comps, cx, cy, nz = d.shape
    n_ent = gcol.shape[0]
    field = pl.BlockSpec((1, cx, cy, nz), lambda f: (f, 0, 0, 0))
    return pl.pallas_call(
        gather_kernel,
        grid=(comps,),
        in_specs=[field, field, pl.BlockSpec(gcol.shape, lambda f: (0, 0))],
        out_specs=pl.BlockSpec((1, 2, 8, n_ent), lambda f: (f, 0, 0, 0)),
        out_shape=jax.ShapeDtypeStruct((comps, 2, 8, n_ent), d.dtype),
        scratch_shapes=[pltpu.VMEM((n_ent, cx * cy), jnp.bfloat16)],
        compiler_params=pltpu.CompilerParams(
            dimension_semantics=("arbitrary",), vmem_limit_bytes=48 * 1024 * 1024
        ),
        cost_estimate=pl.CostEstimate(
            flops=int(2 * 6 * 3 * n_ent * cx * cy * nz), transcendentals=0,
            bytes_accessed=int(8 * comps * cx * cy * nz),
        ),
    )(d, v, gcol)


def update_kernel(d_ref, v_ref, st_ref, m_ref, xm_ref, xp_ref, ym_ref, yp_ref,
                  cols_ref, lanes_ref, vals_ref, gcol_ref, dn_ref, vn_ref, face_ref, g_ref,
                  hot_ref, ghot_ref):
    cx, cy, nz = d_ref.shape[1], d_ref.shape[2], d_ref.shape[3]
    n_cols = cx * cy
    n_ent = cols_ref.shape[1]

    @pl.when(pl.program_id(0) == 0)
    def _():
        col_iota = lax.broadcasted_iota(jnp.int32, (n_cols, n_ent), 0)
        hot_ref[...] = (col_iota == cols_ref[...]).astype(jnp.bfloat16)
        build_ghot(gcol_ref, ghot_ref, n_cols)

    d = d_ref[0]
    xp = jnp.concatenate([d[1:], xp_ref[0][None]], axis=0)
    xm = jnp.concatenate([xm_ref[0][None], d[:-1]], axis=0)
    y_iota = lax.broadcasted_iota(jnp.int32, (cx, cy, nz), 1)
    z_iota = lax.broadcasted_iota(jnp.int32, (cx, cy, nz), 2)
    yp = jnp.where(y_iota == cy - 1, yp_ref[0][:, None, :], pltpu.roll(d, cy - 1, 1))
    ym = jnp.where(y_iota == 0, ym_ref[0][:, None, :], pltpu.roll(d, 1, 1))
    zp = jnp.where(z_iota == nz - 1, 0.0, pltpu.roll(d, nz - 1, 2))
    zm = jnp.where(z_iota == 0, 0.0, pltpu.roll(d, 1, 2))
    lap = xp + xm + yp + ym
    lap = lap + (zp + zm) - 6.0 * d
    internal = st_ref[...] * lap

    lane_hit = lanes_ref[...] == lax.broadcasted_iota(jnp.int32, (nz, n_ent), 0)
    hot = hot_ref[...]
    extra = None
    for part in range(vals_ref.shape[1]):
        w = jnp.where(lane_hit, vals_ref[0, part], 0.0).astype(jnp.bfloat16)
        term = lax.dot_general(
            hot, w, (((1,), (1,)), ((), ())), preferred_element_type=jnp.float32
        )
        extra = term if extra is None else extra + term
    forces = internal + extra.reshape(cx, cy, nz)
    vn = v_ref[0] + TIME_STEP * (forces / m_ref[...])
    vn_ref[0] = vn
    dn = d + TIME_STEP * vn
    dn_ref[0] = dn
    face_ref[0, 0] = dn[0]
    face_ref[0, 1] = dn[cx - 1]
    face_ref[0, 2] = dn_ref[0, :, 0, :]
    face_ref[0, 3] = dn_ref[0, :, cy - 1, :]
    zmask = gcol_ref[:, 1:2] == lax.broadcasted_iota(jnp.int32, (gcol_ref.shape[0], nz), 1)
    gather_rows((dn, vn), ghot_ref[...], zmask, g_ref)


def update_call(d, v, st, m, xm, xp, ym, yp, cols, lanes, vals, gcol):
    comps, cx, cy, nz = d.shape
    n_ent = cols.shape[1]
    field = pl.BlockSpec((1, cx, cy, nz), lambda f: (f, 0, 0, 0))
    plane = pl.BlockSpec((cx, cy, nz), lambda f: (0, 0, 0))
    face = pl.BlockSpec((1, cx, nz), lambda f: (f, 0, 0))
    whole2 = lambda a: pl.BlockSpec(a.shape, lambda f: (0, 0))
    vals_spec = pl.BlockSpec((1,) + vals.shape[1:], lambda f: (f, 0, 0, 0))
    n_el = comps * cx * cy * nz
    cost = pl.CostEstimate(
        flops=int(4 * comps * vals.shape[1] * cx * cy * n_ent * nz + 20 * n_el),
        transcendentals=0,
        bytes_accessed=int(4 * (6 * n_el + 2 * cx * cy * nz)),
    )
    return pl.pallas_call(
        update_kernel,
        grid=(comps,),
        in_specs=[field, field, plane, plane, face, face, face, face,
                  whole2(cols), whole2(lanes), vals_spec, whole2(gcol)],
        out_specs=[field, field, pl.BlockSpec((1, 4, cx, nz), lambda f: (f, 0, 0, 0)),
                   pl.BlockSpec((1, 2, 8, gcol.shape[0]), lambda f: (f, 0, 0, 0))],
        out_shape=[jax.ShapeDtypeStruct(d.shape, d.dtype)] * 2
        + [jax.ShapeDtypeStruct((comps, 4, cx, nz), d.dtype),
           jax.ShapeDtypeStruct((comps, 2, 8, gcol.shape[0]), d.dtype)],
        scratch_shapes=[pltpu.VMEM((cx * cy, n_ent), jnp.bfloat16),
                        pltpu.VMEM((gcol.shape[0], cx * cy), jnp.bfloat16)],
        compiler_params=pltpu.CompilerParams(
            dimension_semantics=("arbitrary",), vmem_limit_bytes=48 * 1024 * 1024
        ),
        cost_estimate=cost,
    )(d, v, st, m, xm, xp, ym, yp, cols, lanes, vals, gcol)


def shift_pairs(axis, up):
    count = lax.axis_size(axis)
    if up:
        return [(i, i + 1) for i in range(count - 1)]
    return [(i + 1, i) for i in range(count - 1)]


def from_partner(value, axis, stride):
    mask = 2**stride
    pairs = [(source, source ^ mask) for source in range(lax.axis_size(axis))]
    return lax.ppermute(value, axis, pairs)


def split3(x):
    hi = lax.reduce_precision(x, exponent_bits=8, mantissa_bits=7)
    rest = x - hi
    mid = lax.reduce_precision(rest, exponent_bits=8, mantissa_bits=7)
    lo = rest - mid
    return jnp.stack([hi, mid, lo]).astype(jnp.bfloat16)


def depth_sum(field):
    zeros = jnp.zeros_like(field[..., :1])
    upper = jnp.concatenate([field[..., 1:], zeros], axis=-1)
    lower = jnp.concatenate([zeros, field[..., :-1]], axis=-1)
    return upper + lower


def local(
    start_disp,
    start_vel,
    stiffness,
    cell_mass,
    contact_cells,
    contact_match,
    eroded_cells,
    owner_ids,
    bed_position,
    bed_velocity,
    bed_neighbours,
):
    cols_x = start_disp.shape[1]
    cols_y = start_disp.shape[2]
    layers = start_disp.shape[3]
    n_cols = cols_x * cols_y
    n_owner = lax.axis_size("gy")
    n_slots = bed_position.shape[3]
    capacity = n_slots // n_owner
    row_block = min(128, n_slots)
    n_blocks = n_slots // row_block
    n_nbr = bed_neighbours.shape[2]
    n_seg = contact_cells.shape[2]
    n_rec = eroded_cells.shape[3]
    col_range = jnp.arange(n_cols, dtype=jnp.int32)
    layer_range = jnp.arange(layers, dtype=jnp.int32)
    seg_hot = (contact_cells[0, 0][:, None] == col_range[None, :]).astype(jnp.float32)
    match_hot = (
        contact_match[0, 0][:, None] == jnp.arange(n_seg, dtype=jnp.int32)[None, :]
    ).astype(jnp.float32)
    local_nbr = bed_neighbours[0, 0].reshape(n_nbr, n_blocks, row_block).transpose(1, 0, 2)
    nbr_hot = (
        local_nbr.reshape(n_blocks, n_nbr * row_block)[..., None]
        == jnp.arange(row_block, dtype=jnp.int32)
    ).astype(jnp.bfloat16)
    nbr_hot = lax.optimization_barrier(nbr_hot)
    owner_range = jnp.arange(n_owner, dtype=jnp.int32)
    rank_range = jnp.arange(capacity, dtype=jnp.int32)
    owners_all = owner_ids[:, 0, 0, :, 0]
    owner_hit = owners_all[..., None] == owner_range
    rec_range = jnp.arange(owner_ids.shape[3], dtype=jnp.int32)
    lower_tri = (rec_range[None, :] <= rec_range[:, None]).astype(jnp.float32)
    counted_all = jnp.einsum(
        "ij,sjo->sio", lower_tri, owner_hit.astype(jnp.float32), precision=HIGHEST
    )
    rank_all = jnp.sum(jnp.where(owner_hit, counted_all, 0.0), axis=-1).astype(jnp.int32) - 1
    is_owner_all = owner_hit.astype(jnp.float32)
    rank_hot_all = (rank_all[..., None] == rank_range).astype(jnp.float32)
    mass_cols = cell_mass.reshape(n_cols, layers)
    n_steps = eroded_cells.shape[0]
    cells_all = eroded_cells[:, 0, 0]
    cc_all = jnp.broadcast_to(contact_cells[0, 0], (n_steps, n_seg))
    ent_cols = jnp.concatenate([cc_all, cells_all // layers], axis=1)[:, None, :]
    ent_lanes = jnp.concatenate(
        [jnp.full((n_steps, n_seg), layers - 1, jnp.int32), cells_all % layers], axis=1
    )[:, None, :]
    gcol_all = jnp.stack([ent_cols[:, 0, :], ent_lanes[:, 0, :]], axis=-1)
    part_pos = bed_position[0, 0]
    part_vel = bed_velocity[0, 0]
    displace = start_disp
    velocity = start_vel
    gath = gather_call(start_disp, start_vel, gcol_all[0])
    faces = jnp.stack(
        [start_disp[:, 0], start_disp[:, -1], start_disp[:, :, 0], start_disp[:, :, -1]], axis=1
    )
    for step_id in range(eroded_cells.shape[0]):
        seg_rows = gath[:, 0, 0, :n_seg]
        rec_disp = gath[:, 0, 0, n_seg:]
        rec_velo = gath[:, 1, 0, n_seg:]
        seg_tile = seg_rows.reshape(3, n_seg // layers, layers)
        up_recv = lax.ppermute(
            jnp.concatenate([faces[:, 1], seg_tile], axis=1), "gx", shift_pairs("gx", True)
        )
        down_recv = lax.ppermute(
            jnp.concatenate([faces[:, 0], seg_tile], axis=1), "gx", shift_pairs("gx", False)
        )
        xm_face = up_recv[:, :cols_x]
        xp_face = down_recv[:, :cols_x]
        ym_face = lax.ppermute(faces[:, 3], "gy", shift_pairs("gy", True))
        yp_face = lax.ppermute(faces[:, 2], "gy", shift_pairs("gy", False))
        partner = jnp.where(
            lax.axis_index("gx") % 2 == 0, down_recv[:, cols_x:], up_recv[:, cols_x:]
        ).reshape(3, n_seg)
        facing = jnp.einsum("fi,ji->fj", partner, match_hot, precision=HIGHEST)
        pull = CONTACT_K * (facing - seg_rows)
        cells_now = eroded_cells[step_id, 0, 0]
        col_hot = ((cells_now // layers)[:, None] == col_range[None, :]).astype(jnp.float32)
        layer_hot = ((cells_now % layers)[:, None] == layer_range[None, :]).astype(jnp.float32)
        mass_rows = jnp.einsum("cz,ec->ez", mass_cols, col_hot, precision=HIGHEST)
        rec_mass = jnp.sum(mass_rows * layer_hot, axis=1)
        rec_mom = rec_mass[None] * rec_velo
        is_owner = is_owner_all[step_id]
        rank_hot = rank_hot_all[step_id]
        state = jnp.concatenate([part_pos, part_vel], axis=0).reshape(6, n_blocks, row_block)
        state_split = split3(state).reshape(3 * 6, n_blocks, row_block)
        gathered = jnp.einsum(
            "pbs,bqs->pbq", state_split, nbr_hot, preferred_element_type=jnp.float32
        ).reshape(3, 6, n_blocks, n_nbr, row_block)
        gathered = gathered[0] + gathered[1] + gathered[2]
        gathered = gathered.transpose(0, 2, 1, 3).reshape(6, n_nbr, n_slots)
        bed_near = gathered[0:3]
        bed_drift = gathered[3:6]
        records = jnp.concatenate([rec_mass[None], rec_disp, rec_mom], axis=0)
        buckets = jnp.einsum("eo,fe,er->ofr", is_owner, records, rank_hot, precision=HIGHEST)
        arrived = lax.all_to_all(buckets, "gy", split_axis=0, concat_axis=0, tiled=True)
        columns = arrived.transpose(1, 2, 0).reshape(7, n_slots)
        slot_mass = columns[0]
        offset = bed_near - columns[1:4][:, None, :]
        weights = 1.0 / (1.0 + jnp.sum(offset * offset, axis=0))
        spring = weights[None] * (PARTICLE_K * slot_mass * offset)
        terms = spring + weights[None] * (
            DRAG_COEF * (slot_mass * bed_drift - columns[4:7][:, None, :])
        )
        slot_force = jnp.sum(terms, axis=1) / n_nbr
        returned = slot_force.reshape(3, capacity, n_owner).transpose(2, 0, 1)
        answers = lax.all_to_all(returned, "gy", split_axis=0, concat_axis=0, tiled=True)
        rec_force = jnp.einsum("ofr,er,eo->fe", answers, rank_hot, is_owner, precision=HIGHEST)
        change = (-TIME_STEP * spring / n_nbr).reshape(3, n_nbr, n_blocks, row_block)
        change = change.transpose(0, 2, 1, 3).reshape(3, n_blocks, n_nbr * row_block)
        change_split = split3(change).reshape(9, n_blocks, n_nbr * row_block)
        vel_add = jnp.einsum(
            "pbq,bqs->pbs", change_split, nbr_hot, preferred_element_type=jnp.float32
        ).reshape(3, 3, n_slots)
        vel_add = vel_add[0] + vel_add[1] + vel_add[2]
        part_vel = part_vel + vel_add
        part_pos = part_pos + TIME_STEP * part_vel
        values = jnp.concatenate([pull, rec_force], axis=1)
        values = split3(values).astype(jnp.float32).transpose(1, 0, 2)[:, :, None, :]
        displace, velocity, faces, gath = update_call(
            displace, velocity, stiffness, cell_mass, xm_face, xp_face, ym_face, yp_face,
            ent_cols[step_id], ent_lanes[step_id], values,
            gcol_all[min(step_id + 1, n_steps - 1)],
        )
    return (displace, velocity)


def solution(mesh):
    return jax.shard_map(
        local,
        mesh=mesh,
        in_specs=(
            P(None, "gx", "gy", None),
            P(None, "gx", "gy", None),
            P("gx", "gy", None),
            P("gx", "gy", None),
            P("gx", "gy", None),
            P("gx", "gy", None),
            P(None, "gx", "gy", None),
            P(None, "gx", "gy", None, None),
            P("gx", "gy", None, None),
            P("gx", "gy", None, None),
            P("gx", "gy", None, None),
        ),
        out_specs=(P(None, "gx", "gy", None), P(None, "gx", "gy", None)),
        check_vma=False,
    )
```

```python
import jax
import jax.numpy as jnp
from jax import lax
from jax.experimental import pallas as pl
from jax.experimental.pallas import tpu as pltpu
from jax.sharding import PartitionSpec as P

TIME_STEP = 0.2
CONTACT_K = 0.5
PARTICLE_K = 1.0
DRAG_COEF = 0.5
HIGHEST = lax.Precision.HIGHEST


def padded_2(cells, sides, width):
    for axis, dim in sides:
        count = lax.axis_size(axis)
        ends = count - 1
        head = lax.slice_in_dim(cells, 0, width, axis=dim)
        tail = lax.slice_in_dim(cells, cells.shape[dim] - width, cells.shape[dim], axis=dim)
        cells = jnp.concatenate(
            [
                lax.ppermute(tail, axis, [(i, (i + 1) % count) for i in range(ends)]),
                cells,
                lax.ppermute(head, axis, [((i + 1) % count, i) for i in range(ends)]),
            ],
            axis=dim,
        )
    return cells


def update_kernel(d_ref, v_ref, st_ref, m_ref, xm_ref, xp_ref, ym_ref, yp_ref,
                  cols_ref, lanes_ref, vals_ref, dn_ref, vn_ref, face_ref, hot_ref):
    cx, cy, nz = d_ref.shape[1], d_ref.shape[2], d_ref.shape[3]
    n_cols = cx * cy
    n_ent = cols_ref.shape[1]

    @pl.when(pl.program_id(0) == 0)
    def _():
        col_iota = lax.broadcasted_iota(jnp.int32, (n_cols, n_ent), 0)
        hot_ref[...] = (col_iota == cols_ref[...]).astype(jnp.bfloat16)

    d = d_ref[0]
    xp = jnp.concatenate([d[1:], xp_ref[0][None]], axis=0)
    xm = jnp.concatenate([xm_ref[0][None], d[:-1]], axis=0)
    y_iota = lax.broadcasted_iota(jnp.int32, (cx, cy, nz), 1)
    z_iota = lax.broadcasted_iota(jnp.int32, (cx, cy, nz), 2)
    yp = jnp.where(y_iota == cy - 1, yp_ref[0][:, None, :], pltpu.roll(d, cy - 1, 1))
    ym = jnp.where(y_iota == 0, ym_ref[0][:, None, :], pltpu.roll(d, 1, 1))
    zp = jnp.where(z_iota == nz - 1, 0.0, pltpu.roll(d, nz - 1, 2))
    zm = jnp.where(z_iota == 0, 0.0, pltpu.roll(d, 1, 2))
    lap = xp + xm + yp + ym
    lap = lap + (zp + zm) - 6.0 * d
    internal = st_ref[...] * lap

    lane_hit = lanes_ref[...] == lax.broadcasted_iota(jnp.int32, (nz, n_ent), 0)
    hot = hot_ref[...]
    extra = None
    for part in range(vals_ref.shape[1]):
        w = jnp.where(lane_hit, vals_ref[0, part], 0.0).astype(jnp.bfloat16)
        term = lax.dot_general(
            hot, w, (((1,), (1,)), ((), ())), preferred_element_type=jnp.float32
        )
        extra = term if extra is None else extra + term
    forces = internal + extra.reshape(cx, cy, nz)
    vn = v_ref[0] + TIME_STEP * (forces / m_ref[...])
    vn_ref[0] = vn
    dn = d + TIME_STEP * vn
    dn_ref[0] = dn
    face_ref[0, 0] = dn[0]
    face_ref[0, 1] = dn[cx - 1]
    face_ref[0, 2] = dn_ref[0, :, 0, :]
    face_ref[0, 3] = dn_ref[0, :, cy - 1, :]


def update_call(d, v, st, m, xm, xp, ym, yp, cols, lanes, vals):
    comps, cx, cy, nz = d.shape
    n_ent = cols.shape[1]
    field = pl.BlockSpec((1, cx, cy, nz), lambda f: (f, 0, 0, 0))
    plane = pl.BlockSpec((cx, cy, nz), lambda f: (0, 0, 0))
    face = pl.BlockSpec((1, cx, nz), lambda f: (f, 0, 0))
    whole2 = lambda a: pl.BlockSpec(a.shape, lambda f: (0, 0))
    vals_spec = pl.BlockSpec((1,) + vals.shape[1:], lambda f: (f, 0, 0, 0))
    n_el = comps * cx * cy * nz
    cost = pl.CostEstimate(
        flops=int(2 * comps * vals.shape[1] * cx * cy * n_ent * nz + 20 * n_el),
        transcendentals=0,
        bytes_accessed=int(4 * (6 * n_el + 2 * cx * cy * nz)),
    )
    return pl.pallas_call(
        update_kernel,
        grid=(comps,),
        in_specs=[field, field, plane, plane, face, face, face, face,
                  whole2(cols), whole2(lanes), vals_spec],
        out_specs=[field, field, pl.BlockSpec((1, 4, cx, nz), lambda f: (f, 0, 0, 0))],
        out_shape=[jax.ShapeDtypeStruct(d.shape, d.dtype)] * 2
        + [jax.ShapeDtypeStruct((comps, 4, cx, nz), d.dtype)],
        scratch_shapes=[pltpu.VMEM((cx * cy, n_ent), jnp.bfloat16)],
        compiler_params=pltpu.CompilerParams(
            dimension_semantics=("arbitrary",), vmem_limit_bytes=48 * 1024 * 1024
        ),
        cost_estimate=cost,
    )(d, v, st, m, xm, xp, ym, yp, cols, lanes, vals)


def shift_pairs(axis, up):
    count = lax.axis_size(axis)
    if up:
        return [(i, i + 1) for i in range(count - 1)]
    return [(i + 1, i) for i in range(count - 1)]


def from_partner(value, axis, stride):
    mask = 2**stride
    pairs = [(source, source ^ mask) for source in range(lax.axis_size(axis))]
    return lax.ppermute(value, axis, pairs)


def split3(x):
    hi = lax.reduce_precision(x, exponent_bits=8, mantissa_bits=7)
    rest = x - hi
    mid = lax.reduce_precision(rest, exponent_bits=8, mantissa_bits=7)
    lo = rest - mid
    return jnp.stack([hi, mid, lo]).astype(jnp.bfloat16)


def depth_sum(field):
    zeros = jnp.zeros_like(field[..., :1])
    upper = jnp.concatenate([field[..., 1:], zeros], axis=-1)
    lower = jnp.concatenate([zeros, field[..., :-1]], axis=-1)
    return upper + lower


def local(
    start_disp,
    start_vel,
    stiffness,
    cell_mass,
    contact_cells,
    contact_match,
    eroded_cells,
    owner_ids,
    bed_position,
    bed_velocity,
    bed_neighbours,
):
    cols_x = start_disp.shape[1]
    cols_y = start_disp.shape[2]
    layers = start_disp.shape[3]
    n_cols = cols_x * cols_y
    n_owner = lax.axis_size("gy")
    n_slots = bed_position.shape[3]
    capacity = n_slots // n_owner
    row_block = min(128, n_slots)
    n_blocks = n_slots // row_block
    n_nbr = bed_neighbours.shape[2]
    n_seg = contact_cells.shape[2]
    n_rec = eroded_cells.shape[3]
    col_range = jnp.arange(n_cols, dtype=jnp.int32)
    layer_range = jnp.arange(layers, dtype=jnp.int32)
    seg_hot = (contact_cells[0, 0][:, None] == col_range[None, :]).astype(jnp.float32)
    match_hot = (
        contact_match[0, 0][:, None] == jnp.arange(n_seg, dtype=jnp.int32)[None, :]
    ).astype(jnp.float32)
    local_nbr = bed_neighbours[0, 0].reshape(n_nbr, n_blocks, row_block).transpose(1, 0, 2)
    nbr_hot = (
        local_nbr.reshape(n_blocks, n_nbr * row_block)[..., None]
        == jnp.arange(row_block, dtype=jnp.int32)
    ).astype(jnp.bfloat16)
    nbr_hot = lax.optimization_barrier(nbr_hot)
    owner_range = jnp.arange(n_owner, dtype=jnp.int32)
    rank_range = jnp.arange(capacity, dtype=jnp.int32)
    owners_all = owner_ids[:, 0, 0, :, 0]
    owner_hit = owners_all[..., None] == owner_range
    rec_range = jnp.arange(owner_ids.shape[3], dtype=jnp.int32)
    lower_tri = (rec_range[None, :] <= rec_range[:, None]).astype(jnp.float32)
    counted_all = jnp.einsum(
        "ij,sjo->sio", lower_tri, owner_hit.astype(jnp.float32), precision=HIGHEST
    )
    rank_all = jnp.sum(jnp.where(owner_hit, counted_all, 0.0), axis=-1).astype(jnp.int32) - 1
    is_owner_all = owner_hit.astype(jnp.float32)
    rank_hot_all = (rank_all[..., None] == rank_range).astype(jnp.float32)
    mass_cols = cell_mass.reshape(n_cols, layers)
    n_steps = eroded_cells.shape[0]
    cells_all = eroded_cells[:, 0, 0]
    cc_all = jnp.broadcast_to(contact_cells[0, 0], (n_steps, n_seg))
    ent_cols = jnp.concatenate([cc_all, cells_all // layers], axis=1)[:, None, :]
    ent_lanes = jnp.concatenate(
        [jnp.full((n_steps, n_seg), layers - 1, jnp.int32), cells_all % layers], axis=1
    )[:, None, :]
    part_pos = bed_position[0, 0]
    part_vel = bed_velocity[0, 0]
    displace = start_disp
    velocity = start_vel
    faces = jnp.stack(
        [start_disp[:, 0], start_disp[:, -1], start_disp[:, :, 0], start_disp[:, :, -1]], axis=1
    )
    for step_id in range(eroded_cells.shape[0]):
        disp_cols = displace.reshape(3, n_cols, layers)
        vel_cols = velocity.reshape(3, n_cols, layers)
        top_layer = disp_cols[:, :, layers - 1]
        seg_rows = jnp.einsum("fc,jc->fj", top_layer, seg_hot, precision=HIGHEST)
        seg_tile = seg_rows.reshape(3, n_seg // layers, layers)
        up_recv = lax.ppermute(
            jnp.concatenate([faces[:, 1], seg_tile], axis=1), "gx", shift_pairs("gx", True)
        )
        down_recv = lax.ppermute(
            jnp.concatenate([faces[:, 0], seg_tile], axis=1), "gx", shift_pairs("gx", False)
        )
        xm_face = up_recv[:, :cols_x]
        xp_face = down_recv[:, :cols_x]
        ym_face = lax.ppermute(faces[:, 3], "gy", shift_pairs("gy", True))
        yp_face = lax.ppermute(faces[:, 2], "gy", shift_pairs("gy", False))
        partner = jnp.where(
            lax.axis_index("gx") % 2 == 0, down_recv[:, cols_x:], up_recv[:, cols_x:]
        ).reshape(3, n_seg)
        facing = jnp.einsum("fi,ji->fj", partner, match_hot, precision=HIGHEST)
        pull = CONTACT_K * (facing - seg_rows)
        cells_now = eroded_cells[step_id, 0, 0]
        col_hot = ((cells_now // layers)[:, None] == col_range[None, :]).astype(jnp.float32)
        layer_hot = ((cells_now % layers)[:, None] == layer_range[None, :]).astype(jnp.float32)
        stacked = jnp.concatenate([mass_cols[None], disp_cols, vel_cols], axis=0)
        picked_cols = jnp.einsum("fcz,ec->fez", stacked, col_hot, precision=HIGHEST)
        picked = jnp.sum(picked_cols * layer_hot[None], axis=2)
        rec_mass = picked[0]
        rec_disp = picked[1:4]
        rec_mom = rec_mass[None] * picked[4:7]
        is_owner = is_owner_all[step_id]
        rank_hot = rank_hot_all[step_id]
        state = jnp.concatenate([part_pos, part_vel], axis=0).reshape(6, n_blocks, row_block)
        state_split = split3(state).reshape(3 * 6, n_blocks, row_block)
        gathered = jnp.einsum(
            "pbs,bqs->pbq", state_split, nbr_hot, preferred_element_type=jnp.float32
        ).reshape(3, 6, n_blocks, n_nbr, row_block)
        gathered = gathered[0] + gathered[1] + gathered[2]
        gathered = gathered.transpose(0, 2, 1, 3).reshape(6, n_nbr, n_slots)
        bed_near = gathered[0:3]
        bed_drift = gathered[3:6]
        records = jnp.concatenate([rec_mass[None], rec_disp, rec_mom], axis=0)
        buckets = jnp.einsum("eo,fe,er->ofr", is_owner, records, rank_hot, precision=HIGHEST)
        arrived = lax.all_to_all(buckets, "gy", split_axis=0, concat_axis=0, tiled=True)
        columns = arrived.transpose(1, 2, 0).reshape(7, n_slots)
        slot_mass = columns[0]
        offset = bed_near - columns[1:4][:, None, :]
        weights = 1.0 / (1.0 + jnp.sum(offset * offset, axis=0))
        spring = weights[None] * (PARTICLE_K * slot_mass * offset)
        terms = spring + weights[None] * (
            DRAG_COEF * (slot_mass * bed_drift - columns[4:7][:, None, :])
        )
        slot_force = jnp.sum(terms, axis=1) / n_nbr
        returned = slot_force.reshape(3, capacity, n_owner).transpose(2, 0, 1)
        answers = lax.all_to_all(returned, "gy", split_axis=0, concat_axis=0, tiled=True)
        rec_force = jnp.einsum("ofr,er,eo->fe", answers, rank_hot, is_owner, precision=HIGHEST)
        change = (-TIME_STEP * spring / n_nbr).reshape(3, n_nbr, n_blocks, row_block)
        change = change.transpose(0, 2, 1, 3).reshape(3, n_blocks, n_nbr * row_block)
        change_split = split3(change).reshape(9, n_blocks, n_nbr * row_block)
        vel_add = jnp.einsum(
            "pbq,bqs->pbs", change_split, nbr_hot, preferred_element_type=jnp.float32
        ).reshape(3, 3, n_slots)
        vel_add = vel_add[0] + vel_add[1] + vel_add[2]
        part_vel = part_vel + vel_add
        part_pos = part_pos + TIME_STEP * part_vel
        values = jnp.concatenate([pull, rec_force], axis=1)
        values = split3(values).astype(jnp.float32).transpose(1, 0, 2)[:, :, None, :]
        displace, velocity, faces = update_call(
            displace, velocity, stiffness, cell_mass, xm_face, xp_face, ym_face, yp_face,
            ent_cols[step_id], ent_lanes[step_id], values,
        )
    return (displace, velocity)


def solution(mesh):
    return jax.shard_map(
        local,
        mesh=mesh,
        in_specs=(
            P(None, "gx", "gy", None),
            P(None, "gx", "gy", None),
            P("gx", "gy", None),
            P("gx", "gy", None),
            P("gx", "gy", None),
            P("gx", "gy", None),
            P(None, "gx", "gy", None),
            P(None, "gx", "gy", None, None),
            P("gx", "gy", None, None),
            P("gx", "gy", None, None),
            P("gx", "gy", None, None),
        ),
        out_specs=(P(None, "gx", "gy", None), P(None, "gx", "gy", None)),
        check_vma=False,
    )
```

```python
import jax
import jax.numpy as jnp
from jax import lax
from jax.experimental import pallas as pl
from jax.experimental.pallas import tpu as pltpu
from jax.sharding import PartitionSpec as P

TIME_STEP = 0.2
CONTACT_K = 0.5
PARTICLE_K = 1.0
DRAG_COEF = 0.5
HIGHEST = lax.Precision.HIGHEST


def padded_2(cells, sides, width):
    for axis, dim in sides:
        count = lax.axis_size(axis)
        ends = count - 1
        head = lax.slice_in_dim(cells, 0, width, axis=dim)
        tail = lax.slice_in_dim(cells, cells.shape[dim] - width, cells.shape[dim], axis=dim)
        cells = jnp.concatenate(
            [
                lax.ppermute(tail, axis, [(i, (i + 1) % count) for i in range(ends)]),
                cells,
                lax.ppermute(head, axis, [((i + 1) % count, i) for i in range(ends)]),
            ],
            axis=dim,
        )
    return cells


def update_kernel(d_ref, v_ref, sm_ref, xm_ref, xp_ref, ym_ref, yp_ref,
                  cols_ref, lanes_ref, vals_ref, dn_ref, vn_ref, face_ref, hot_ref):
    cx, cy, nz = d_ref.shape[1], d_ref.shape[2], d_ref.shape[3]
    n_cols = cx * cy
    n_ent = cols_ref.shape[1]

    @pl.when(pl.program_id(0) == 0)
    def _():
        col_iota = lax.broadcasted_iota(jnp.int32, (n_cols, n_ent), 0)
        hot_ref[...] = (col_iota == cols_ref[...]).astype(jnp.bfloat16)

    d = d_ref[0]
    xp = jnp.concatenate([d[1:], xp_ref[0][None]], axis=0)
    xm = jnp.concatenate([xm_ref[0][None], d[:-1]], axis=0)
    y_iota = lax.broadcasted_iota(jnp.int32, (cx, cy, nz), 1)
    z_iota = lax.broadcasted_iota(jnp.int32, (cx, cy, nz), 2)
    yp = jnp.where(y_iota == cy - 1, yp_ref[0][:, None, :], pltpu.roll(d, cy - 1, 1))
    ym = jnp.where(y_iota == 0, ym_ref[0][:, None, :], pltpu.roll(d, 1, 1))
    zp = jnp.where(z_iota == nz - 1, 0.0, pltpu.roll(d, nz - 1, 2))
    zm = jnp.where(z_iota == 0, 0.0, pltpu.roll(d, 1, 2))
    lap = xp + xm + yp + ym
    lap = lap + (zp + zm) - 6.0 * d
    internal = sm_ref[0] * lap

    lane_hit = lanes_ref[...] == lax.broadcasted_iota(jnp.int32, (nz, n_ent), 0)
    hot = hot_ref[...]
    extra = None
    for part in range(vals_ref.shape[1]):
        w = jnp.where(lane_hit, vals_ref[0, part], 0.0).astype(jnp.bfloat16)
        term = lax.dot_general(
            hot, w, (((1,), (1,)), ((), ())), preferred_element_type=jnp.float32
        )
        extra = term if extra is None else extra + term
    forces = internal + extra.reshape(cx, cy, nz)
    vn = v_ref[0] + TIME_STEP * (forces / sm_ref[1])
    vn_ref[0] = vn
    dn = d + TIME_STEP * vn
    dn_ref[0] = dn
    face_ref[0, 0] = dn[0]
    face_ref[0, 1] = dn[cx - 1]
    face_ref[0, 2] = dn_ref[0, :, 0, :]
    face_ref[0, 3] = dn_ref[0, :, cy - 1, :]


def update_call(d, v, sm, xm, xp, ym, yp, cols, lanes, vals):
    comps, cx, cy, nz = d.shape
    n_ent = cols.shape[1]
    field = pl.BlockSpec((1, cx, cy, nz), lambda f: (f, 0, 0, 0))
    plane = pl.BlockSpec((2, cx, cy, nz), lambda f: (0, 0, 0, 0))
    face = pl.BlockSpec((1, cx, nz), lambda f: (f, 0, 0))
    whole2 = lambda a: pl.BlockSpec(a.shape, lambda f: (0, 0))
    vals_spec = pl.BlockSpec((1,) + vals.shape[1:], lambda f: (f, 0, 0, 0))
    n_el = comps * cx * cy * nz
    cost = pl.CostEstimate(
        flops=int(2 * comps * vals.shape[1] * cx * cy * n_ent * nz + 20 * n_el),
        transcendentals=0,
        bytes_accessed=int(4 * (6 * n_el + 2 * cx * cy * nz)),
    )
    return pl.pallas_call(
        update_kernel,
        grid=(comps,),
        in_specs=[field, field, plane, face, face, face, face,
                  whole2(cols), whole2(lanes), vals_spec],
        out_specs=[field, field, pl.BlockSpec((1, 4, cx, nz), lambda f: (f, 0, 0, 0))],
        out_shape=[jax.ShapeDtypeStruct(d.shape, d.dtype)] * 2
        + [jax.ShapeDtypeStruct((comps, 4, cx, nz), d.dtype)],
        scratch_shapes=[pltpu.VMEM((cx * cy, n_ent), jnp.bfloat16)],
        compiler_params=pltpu.CompilerParams(
            dimension_semantics=("arbitrary",), vmem_limit_bytes=48 * 1024 * 1024
        ),
        cost_estimate=cost,
    )(d, v, sm, xm, xp, ym, yp, cols, lanes, vals)


def shift_pairs(axis, up):
    count = lax.axis_size(axis)
    if up:
        return [(i, i + 1) for i in range(count - 1)]
    return [(i + 1, i) for i in range(count - 1)]


def from_partner(value, axis, stride):
    mask = 2**stride
    pairs = [(source, source ^ mask) for source in range(lax.axis_size(axis))]
    return lax.ppermute(value, axis, pairs)


def split3(x):
    hi = lax.reduce_precision(x, exponent_bits=8, mantissa_bits=7)
    rest = x - hi
    mid = lax.reduce_precision(rest, exponent_bits=8, mantissa_bits=7)
    lo = rest - mid
    return jnp.stack([hi, mid, lo]).astype(jnp.bfloat16)


def depth_sum(field):
    zeros = jnp.zeros_like(field[..., :1])
    upper = jnp.concatenate([field[..., 1:], zeros], axis=-1)
    lower = jnp.concatenate([zeros, field[..., :-1]], axis=-1)
    return upper + lower


def local(
    start_disp,
    start_vel,
    stiffness,
    cell_mass,
    contact_cells,
    contact_match,
    eroded_cells,
    owner_ids,
    bed_position,
    bed_velocity,
    bed_neighbours,
):
    cols_x = start_disp.shape[1]
    cols_y = start_disp.shape[2]
    layers = start_disp.shape[3]
    n_cols = cols_x * cols_y
    n_owner = lax.axis_size("gy")
    n_slots = bed_position.shape[3]
    capacity = n_slots // n_owner
    row_block = min(128, n_slots)
    n_blocks = n_slots // row_block
    n_nbr = bed_neighbours.shape[2]
    n_seg = contact_cells.shape[2]
    n_rec = eroded_cells.shape[3]
    col_range = jnp.arange(n_cols, dtype=jnp.int32)
    layer_range = jnp.arange(layers, dtype=jnp.int32)
    seg_hot = (contact_cells[0, 0][:, None] == col_range[None, :]).astype(jnp.float32)
    match_hot = (
        contact_match[0, 0][:, None] == jnp.arange(n_seg, dtype=jnp.int32)[None, :]
    ).astype(jnp.float32)
    local_nbr = bed_neighbours[0, 0].reshape(n_nbr, n_blocks, row_block).transpose(1, 0, 2)
    nbr_hot = (
        local_nbr.reshape(n_blocks, n_nbr * row_block)[..., None]
        == jnp.arange(row_block, dtype=jnp.int32)
    ).astype(jnp.bfloat16)
    nbr_hot = lax.optimization_barrier(nbr_hot)
    owner_range = jnp.arange(n_owner, dtype=jnp.int32)
    rank_range = jnp.arange(capacity, dtype=jnp.int32)
    owners_all = owner_ids[:, 0, 0, :, 0]
    owner_hit = owners_all[..., None] == owner_range
    rec_range = jnp.arange(owner_ids.shape[3], dtype=jnp.int32)
    lower_tri = (rec_range[None, :] <= rec_range[:, None]).astype(jnp.float32)
    counted_all = jnp.einsum(
        "ij,sjo->sio", lower_tri, owner_hit.astype(jnp.float32), precision=HIGHEST
    )
    rank_all = jnp.sum(jnp.where(owner_hit, counted_all, 0.0), axis=-1).astype(jnp.int32) - 1
    is_owner_all = owner_hit.astype(jnp.float32)
    rank_hot_all = (rank_all[..., None] == rank_range).astype(jnp.float32)
    mass_cols = cell_mass.reshape(n_cols, layers)
    n_steps = eroded_cells.shape[0]
    cells_all = eroded_cells[:, 0, 0]
    cc_all = jnp.broadcast_to(contact_cells[0, 0], (n_steps, n_seg))
    ent_cols = jnp.concatenate([cc_all, cells_all // layers], axis=1)[:, None, :]
    ent_lanes = jnp.concatenate(
        [jnp.full((n_steps, n_seg), layers - 1, jnp.int32), cells_all % layers], axis=1
    )[:, None, :]
    part_pos = bed_position[0, 0]
    part_vel = bed_velocity[0, 0]
    displace = start_disp
    velocity = start_vel
    stiff_mass = jnp.stack([stiffness, cell_mass])
    faces = jnp.stack(
        [start_disp[:, 0], start_disp[:, -1], start_disp[:, :, 0], start_disp[:, :, -1]], axis=1
    )
    for step_id in range(eroded_cells.shape[0]):
        xm_face = lax.ppermute(faces[:, 1], "gx", shift_pairs("gx", True))
        xp_face = lax.ppermute(faces[:, 0], "gx", shift_pairs("gx", False))
        ym_face = lax.ppermute(faces[:, 3], "gy", shift_pairs("gy", True))
        yp_face = lax.ppermute(faces[:, 2], "gy", shift_pairs("gy", False))
        disp_cols = displace.reshape(3, n_cols, layers)
        vel_cols = velocity.reshape(3, n_cols, layers)
        top_layer = disp_cols[:, :, layers - 1]
        seg_rows = jnp.einsum("fc,jc->fj", top_layer, seg_hot, precision=HIGHEST)
        partner = from_partner(seg_rows, "gx", 0)
        facing = jnp.einsum("fi,ji->fj", partner, match_hot, precision=HIGHEST)
        pull = CONTACT_K * (facing - seg_rows)
        cells_now = eroded_cells[step_id, 0, 0]
        col_hot = ((cells_now // layers)[:, None] == col_range[None, :]).astype(jnp.float32)
        layer_hot = ((cells_now % layers)[:, None] == layer_range[None, :]).astype(jnp.float32)
        stacked = jnp.concatenate([mass_cols[None], disp_cols, vel_cols], axis=0)
        picked_cols = jnp.einsum("fcz,ec->fez", stacked, col_hot, precision=HIGHEST)
        picked = jnp.sum(picked_cols * layer_hot[None], axis=2)
        rec_mass = picked[0]
        rec_disp = picked[1:4]
        rec_mom = rec_mass[None] * picked[4:7]
        is_owner = is_owner_all[step_id]
        rank_hot = rank_hot_all[step_id]
        state = jnp.concatenate([part_pos, part_vel], axis=0).reshape(6, n_blocks, row_block)
        state_split = split3(state).reshape(3 * 6, n_blocks, row_block)
        gathered = jnp.einsum(
            "pbs,bqs->pbq", state_split, nbr_hot, preferred_element_type=jnp.float32
        ).reshape(3, 6, n_blocks, n_nbr, row_block)
        gathered = gathered[0] + gathered[1] + gathered[2]
        gathered = gathered.transpose(0, 2, 1, 3).reshape(6, n_nbr, n_slots)
        bed_near = gathered[0:3]
        bed_drift = gathered[3:6]
        records = jnp.concatenate([rec_mass[None], rec_disp, rec_mom], axis=0)
        buckets = jnp.einsum("eo,fe,er->ofr", is_owner, records, rank_hot, precision=HIGHEST)
        arrived = lax.all_to_all(buckets, "gy", split_axis=0, concat_axis=0, tiled=True)
        columns = arrived.transpose(1, 2, 0).reshape(7, n_slots)
        slot_mass = columns[0]
        offset = bed_near - columns[1:4][:, None, :]
        weights = 1.0 / (1.0 + jnp.sum(offset * offset, axis=0))
        spring = weights[None] * (PARTICLE_K * slot_mass * offset)
        terms = spring + weights[None] * (
            DRAG_COEF * (slot_mass * bed_drift - columns[4:7][:, None, :])
        )
        slot_force = jnp.sum(terms, axis=1) / n_nbr
        returned = slot_force.reshape(3, capacity, n_owner).transpose(2, 0, 1)
        answers = lax.all_to_all(returned, "gy", split_axis=0, concat_axis=0, tiled=True)
        rec_force = jnp.einsum("ofr,er,eo->fe", answers, rank_hot, is_owner, precision=HIGHEST)
        change = (-TIME_STEP * spring / n_nbr).reshape(3, n_nbr, n_blocks, row_block)
        change = change.transpose(0, 2, 1, 3).reshape(3, n_blocks, n_nbr * row_block)
        change_split = split3(change).reshape(9, n_blocks, n_nbr * row_block)
        vel_add = jnp.einsum(
            "pbq,bqs->pbs", change_split, nbr_hot, preferred_element_type=jnp.float32
        ).reshape(3, 3, n_slots)
        vel_add = vel_add[0] + vel_add[1] + vel_add[2]
        part_vel = part_vel + vel_add
        part_pos = part_pos + TIME_STEP * part_vel
        values = jnp.concatenate([pull, rec_force], axis=1)
        values = split3(values).astype(jnp.float32).transpose(1, 0, 2)[:, :, None, :]
        displace, velocity, faces = update_call(
            displace, velocity, stiff_mass, xm_face, xp_face, ym_face, yp_face,
            ent_cols[step_id], ent_lanes[step_id], values,
        )
    return (displace, velocity)


def solution(mesh):
    return jax.shard_map(
        local,
        mesh=mesh,
        in_specs=(
            P(None, "gx", "gy", None),
            P(None, "gx", "gy", None),
            P("gx", "gy", None),
            P("gx", "gy", None),
            P("gx", "gy", None),
            P("gx", "gy", None),
            P(None, "gx", "gy", None),
            P(None, "gx", "gy", None, None),
            P("gx", "gy", None, None),
            P("gx", "gy", None, None),
            P("gx", "gy", None, None),
        ),
        out_specs=(P(None, "gx", "gy", None), P(None, "gx", "gy", None)),
        check_vma=False,
    )
```

```python
import jax
import jax.numpy as jnp
from jax import lax
from jax.experimental import pallas as pl
from jax.experimental.pallas import tpu as pltpu
from jax.sharding import PartitionSpec as P

TIME_STEP = 0.2
CONTACT_K = 0.5
PARTICLE_K = 1.0
DRAG_COEF = 0.5
HIGHEST = lax.Precision.HIGHEST


def padded_2(cells, sides, width):
    for axis, dim in sides:
        count = lax.axis_size(axis)
        ends = count - 1
        head = lax.slice_in_dim(cells, 0, width, axis=dim)
        tail = lax.slice_in_dim(cells, cells.shape[dim] - width, cells.shape[dim], axis=dim)
        cells = jnp.concatenate(
            [
                lax.ppermute(tail, axis, [(i, (i + 1) % count) for i in range(ends)]),
                cells,
                lax.ppermute(head, axis, [((i + 1) % count, i) for i in range(ends)]),
            ],
            axis=dim,
        )
    return cells


def update_kernel(d_ref, v_ref, sm_ref, fc_ref,
                  cols_ref, lanes_ref, vals_ref, dn_ref, vn_ref, face_ref, hot_ref):
    cx, cy, nz = d_ref.shape[1], d_ref.shape[2], d_ref.shape[3]
    n_cols = cx * cy
    n_ent = cols_ref.shape[1]

    @pl.when(pl.program_id(0) == 0)
    def _():
        col_iota = lax.broadcasted_iota(jnp.int32, (n_cols, n_ent), 0)
        hot_ref[...] = (col_iota == cols_ref[...]).astype(jnp.bfloat16)

    d = d_ref[0]
    xp = jnp.concatenate([d[1:], fc_ref[1, 0][None]], axis=0)
    xm = jnp.concatenate([fc_ref[0, 0][None], d[:-1]], axis=0)
    y_iota = lax.broadcasted_iota(jnp.int32, (cx, cy, nz), 1)
    z_iota = lax.broadcasted_iota(jnp.int32, (cx, cy, nz), 2)
    yp = jnp.where(y_iota == cy - 1, fc_ref[3, 0][:, None, :], pltpu.roll(d, cy - 1, 1))
    ym = jnp.where(y_iota == 0, fc_ref[2, 0][:, None, :], pltpu.roll(d, 1, 1))
    zp = jnp.where(z_iota == nz - 1, 0.0, pltpu.roll(d, nz - 1, 2))
    zm = jnp.where(z_iota == 0, 0.0, pltpu.roll(d, 1, 2))
    lap = xp + xm + yp + ym
    lap = lap + (zp + zm) - 6.0 * d
    internal = sm_ref[0] * lap

    lane_hit = lanes_ref[...] == lax.broadcasted_iota(jnp.int32, (nz, n_ent), 0)
    hot = hot_ref[...]
    extra = None
    for part in range(vals_ref.shape[1]):
        w = jnp.where(lane_hit, vals_ref[0, part], 0.0).astype(jnp.bfloat16)
        term = lax.dot_general(
            hot, w, (((1,), (1,)), ((), ())), preferred_element_type=jnp.float32
        )
        extra = term if extra is None else extra + term
    forces = internal + extra.reshape(cx, cy, nz)
    vn = v_ref[0] + TIME_STEP * (forces / sm_ref[1])
    vn_ref[0] = vn
    dn = d + TIME_STEP * vn
    dn_ref[0] = dn
    face_ref[0, 0] = dn[0]
    face_ref[0, 1] = dn[cx - 1]
    face_ref[0, 2] = dn_ref[0, :, 0, :]
    face_ref[0, 3] = dn_ref[0, :, cy - 1, :]


def update_call(d, v, sm, fc, cols, lanes, vals):
    comps, cx, cy, nz = d.shape
    n_ent = cols.shape[1]
    field = pl.BlockSpec((1, cx, cy, nz), lambda f: (f, 0, 0, 0))
    plane = pl.BlockSpec((2, cx, cy, nz), lambda f: (0, 0, 0, 0))
    face = pl.BlockSpec((4, 1, cx, nz), lambda f: (0, f, 0, 0))
    whole2 = lambda a: pl.BlockSpec(a.shape, lambda f: (0, 0))
    vals_spec = pl.BlockSpec((1,) + vals.shape[1:], lambda f: (f, 0, 0, 0))
    n_el = comps * cx * cy * nz
    cost = pl.CostEstimate(
        flops=int(2 * comps * vals.shape[1] * cx * cy * n_ent * nz + 20 * n_el),
        transcendentals=0,
        bytes_accessed=int(4 * (6 * n_el + 2 * cx * cy * nz)),
    )
    return pl.pallas_call(
        update_kernel,
        grid=(comps,),
        in_specs=[field, field, plane, face,
                  whole2(cols), whole2(lanes), vals_spec],
        out_specs=[field, field, pl.BlockSpec((1, 4, cx, nz), lambda f: (f, 0, 0, 0))],
        out_shape=[jax.ShapeDtypeStruct(d.shape, d.dtype)] * 2
        + [jax.ShapeDtypeStruct((comps, 4, cx, nz), d.dtype)],
        scratch_shapes=[pltpu.VMEM((cx * cy, n_ent), jnp.bfloat16)],
        compiler_params=pltpu.CompilerParams(
            dimension_semantics=("arbitrary",), vmem_limit_bytes=48 * 1024 * 1024
        ),
        cost_estimate=cost,
    )(d, v, sm, fc, cols, lanes, vals)


def shift_pairs(axis, up):
    count = lax.axis_size(axis)
    if up:
        return [(i, i + 1) for i in range(count - 1)]
    return [(i + 1, i) for i in range(count - 1)]


def from_partner(value, axis, stride):
    mask = 2**stride
    pairs = [(source, source ^ mask) for source in range(lax.axis_size(axis))]
    return lax.ppermute(value, axis, pairs)


def split3(x):
    hi = lax.reduce_precision(x, exponent_bits=8, mantissa_bits=7)
    rest = x - hi
    mid = lax.reduce_precision(rest, exponent_bits=8, mantissa_bits=7)
    lo = rest - mid
    return jnp.stack([hi, mid, lo]).astype(jnp.bfloat16)


def depth_sum(field):
    zeros = jnp.zeros_like(field[..., :1])
    upper = jnp.concatenate([field[..., 1:], zeros], axis=-1)
    lower = jnp.concatenate([zeros, field[..., :-1]], axis=-1)
    return upper + lower


def local(
    start_disp,
    start_vel,
    stiffness,
    cell_mass,
    contact_cells,
    contact_match,
    eroded_cells,
    owner_ids,
    bed_position,
    bed_velocity,
    bed_neighbours,
):
    cols_x = start_disp.shape[1]
    cols_y = start_disp.shape[2]
    layers = start_disp.shape[3]
    n_cols = cols_x * cols_y
    n_owner = lax.axis_size("gy")
    n_slots = bed_position.shape[3]
    capacity = n_slots // n_owner
    row_block = min(128, n_slots)
    n_blocks = n_slots // row_block
    n_nbr = bed_neighbours.shape[2]
    n_seg = contact_cells.shape[2]
    n_rec = eroded_cells.shape[3]
    col_range = jnp.arange(n_cols, dtype=jnp.int32)
    layer_range = jnp.arange(layers, dtype=jnp.int32)
    seg_hot = (contact_cells[0, 0][:, None] == col_range[None, :]).astype(jnp.float32)
    match_hot = (
        contact_match[0, 0][:, None] == jnp.arange(n_seg, dtype=jnp.int32)[None, :]
    ).astype(jnp.float32)
    local_nbr = bed_neighbours[0, 0].reshape(n_nbr, n_blocks, row_block).transpose(1, 0, 2)
    nbr_hot = (
        local_nbr.reshape(n_blocks, n_nbr * row_block)[..., None]
        == jnp.arange(row_block, dtype=jnp.int32)
    ).astype(jnp.bfloat16)
    nbr_hot = lax.optimization_barrier(nbr_hot)
    owner_range = jnp.arange(n_owner, dtype=jnp.int32)
    rank_range = jnp.arange(capacity, dtype=jnp.int32)
    owners_all = owner_ids[:, 0, 0, :, 0]
    owner_hit = owners_all[..., None] == owner_range
    rec_range = jnp.arange(owner_ids.shape[3], dtype=jnp.int32)
    lower_tri = (rec_range[None, :] <= rec_range[:, None]).astype(jnp.float32)
    counted_all = jnp.einsum(
        "ij,sjo->sio", lower_tri, owner_hit.astype(jnp.float32), precision=HIGHEST
    )
    rank_all = jnp.sum(jnp.where(owner_hit, counted_all, 0.0), axis=-1).astype(jnp.int32) - 1
    is_owner_all = owner_hit.astype(jnp.float32)
    rank_hot_all = (rank_all[..., None] == rank_range).astype(jnp.float32)
    mass_cols = cell_mass.reshape(n_cols, layers)
    n_steps = eroded_cells.shape[0]
    cells_all = eroded_cells[:, 0, 0]
    cc_all = jnp.broadcast_to(contact_cells[0, 0], (n_steps, n_seg))
    ent_cols = jnp.concatenate([cc_all, cells_all // layers], axis=1)[:, None, :]
    ent_lanes = jnp.concatenate(
        [jnp.full((n_steps, n_seg), layers - 1, jnp.int32), cells_all % layers], axis=1
    )[:, None, :]
    part_pos = bed_position[0, 0]
    part_vel = bed_velocity[0, 0]
    displace = start_disp
    velocity = start_vel
    stiff_mass = jnp.stack([stiffness, cell_mass])
    faces = jnp.stack(
        [start_disp[:, 0], start_disp[:, -1], start_disp[:, :, 0], start_disp[:, :, -1]], axis=1
    )
    for step_id in range(eroded_cells.shape[0]):
        xm_face = lax.ppermute(faces[:, 1], "gx", shift_pairs("gx", True))
        xp_face = lax.ppermute(faces[:, 0], "gx", shift_pairs("gx", False))
        ym_face = lax.ppermute(faces[:, 3], "gy", shift_pairs("gy", True))
        yp_face = lax.ppermute(faces[:, 2], "gy", shift_pairs("gy", False))
        disp_cols = displace.reshape(3, n_cols, layers)
        vel_cols = velocity.reshape(3, n_cols, layers)
        top_layer = disp_cols[:, :, layers - 1]
        seg_rows = jnp.einsum("fc,jc->fj", top_layer, seg_hot, precision=HIGHEST)
        partner = from_partner(seg_rows, "gx", 0)
        facing = jnp.einsum("fi,ji->fj", partner, match_hot, precision=HIGHEST)
        pull = CONTACT_K * (facing - seg_rows)
        cells_now = eroded_cells[step_id, 0, 0]
        col_hot = ((cells_now // layers)[:, None] == col_range[None, :]).astype(jnp.float32)
        layer_hot = ((cells_now % layers)[:, None] == layer_range[None, :]).astype(jnp.float32)
        stacked = jnp.concatenate([mass_cols[None], disp_cols, vel_cols], axis=0)
        picked_cols = jnp.einsum("fcz,ec->fez", stacked, col_hot, precision=HIGHEST)
        picked = jnp.sum(picked_cols * layer_hot[None], axis=2)
        rec_mass = picked[0]
        rec_disp = picked[1:4]
        rec_mom = rec_mass[None] * picked[4:7]
        is_owner = is_owner_all[step_id]
        rank_hot = rank_hot_all[step_id]
        state = jnp.concatenate([part_pos, part_vel], axis=0).reshape(6, n_blocks, row_block)
        state_split = split3(state).reshape(3 * 6, n_blocks, row_block)
        gathered = jnp.einsum(
            "pbs,bqs->pbq", state_split, nbr_hot, preferred_element_type=jnp.float32
        ).reshape(3, 6, n_blocks, n_nbr, row_block)
        gathered = gathered[0] + gathered[1] + gathered[2]
        gathered = gathered.transpose(0, 2, 1, 3).reshape(6, n_nbr, n_slots)
        bed_near = gathered[0:3]
        bed_drift = gathered[3:6]
        records = jnp.concatenate([rec_mass[None], rec_disp, rec_mom], axis=0)
        buckets = jnp.einsum("eo,fe,er->ofr", is_owner, records, rank_hot, precision=HIGHEST)
        arrived = lax.all_to_all(buckets, "gy", split_axis=0, concat_axis=0, tiled=True)
        columns = arrived.transpose(1, 2, 0).reshape(7, n_slots)
        slot_mass = columns[0]
        offset = bed_near - columns[1:4][:, None, :]
        weights = 1.0 / (1.0 + jnp.sum(offset * offset, axis=0))
        spring = weights[None] * (PARTICLE_K * slot_mass * offset)
        terms = spring + weights[None] * (
            DRAG_COEF * (slot_mass * bed_drift - columns[4:7][:, None, :])
        )
        slot_force = jnp.sum(terms, axis=1) / n_nbr
        returned = slot_force.reshape(3, capacity, n_owner).transpose(2, 0, 1)
        answers = lax.all_to_all(returned, "gy", split_axis=0, concat_axis=0, tiled=True)
        rec_force = jnp.einsum("ofr,er,eo->fe", answers, rank_hot, is_owner, precision=HIGHEST)
        change = (-TIME_STEP * spring / n_nbr).reshape(3, n_nbr, n_blocks, row_block)
        change = change.transpose(0, 2, 1, 3).reshape(3, n_blocks, n_nbr * row_block)
        change_split = split3(change).reshape(9, n_blocks, n_nbr * row_block)
        vel_add = jnp.einsum(
            "pbq,bqs->pbs", change_split, nbr_hot, preferred_element_type=jnp.float32
        ).reshape(3, 3, n_slots)
        vel_add = vel_add[0] + vel_add[1] + vel_add[2]
        part_vel = part_vel + vel_add
        part_pos = part_pos + TIME_STEP * part_vel
        values = jnp.concatenate([pull, rec_force], axis=1)
        values = split3(values).astype(jnp.float32).transpose(1, 0, 2)[:, :, None, :]
        displace, velocity, faces = update_call(
            displace, velocity, stiff_mass, jnp.stack([xm_face, xp_face, ym_face, yp_face]),
            ent_cols[step_id], ent_lanes[step_id], values,
        )
    return (displace, velocity)


def solution(mesh):
    return jax.shard_map(
        local,
        mesh=mesh,
        in_specs=(
            P(None, "gx", "gy", None),
            P(None, "gx", "gy", None),
            P("gx", "gy", None),
            P("gx", "gy", None),
            P("gx", "gy", None),
            P("gx", "gy", None),
            P(None, "gx", "gy", None),
            P(None, "gx", "gy", None, None),
            P("gx", "gy", None, None),
            P("gx", "gy", None, None),
            P("gx", "gy", None, None),
        ),
        out_specs=(P(None, "gx", "gy", None), P(None, "gx", "gy", None)),
        check_vma=False,
    )
```
